32 devices in a mesh: member: 8 (over z, core), lat: 4 (over y, x).
Axes of the slice: x: 2, y: 2, z: 4, core: 2. Of those that a mesh axis runs over, the one named last changes fastest.
Arguments:
- latents: bfloat16 [8, 12, 45, 720], P('member', 'lat'), may hold values from -6 to 6
- filters: bfloat16 [5, 45, 45], replicated, may hold values from -0.125 to 0.125
- project: bfloat16 [5, 45], replicated, may hold values from -0.875 to 0.875
- subcell_maps: bfloat16 [4, 5, 5], replicated, may hold values from -2.5 to 2.5
- verifying_truth: float32 [4, 5, 12, 720], P(None, None, 'lat', 'member'), may hold values from -6 to 6
- basis_rows: int32 [12, 49], replicated, may hold values from 0 to 5
- step_rows: int32 [12], replicated, may hold values from 1 to 3
Outputs:
- d_latent: bfloat16 [8, 12, 45, 720], P('member', 'lat')
The draws below stay inside these ranges and needn't reach their ends.
Inputs may be any that keep to these rules, and one draw needn't show every extreme that they name: `basis_rows`: the value 5 marks a tap outside the filter's support; smaller values name a basis filter.
All inputs are finite; a program needn't handle non-finite values.
Results may differ from the reference program's by a relative error of at most 0.0077.
Values may be sent and summed in bfloat16 or wider, within the bound.
No kernel may reach another device: no remote copies, remote signals or barrier semaphores. Data moves between devices by JAX's collectives and lax.ppermute only.
A program may use at most 64 MiB of HBM per device.

```python
import jax
import jax.numpy as jnp
from jax import lax

C = 45
V = 5
K = 5
W = 720
ENSEMBLE_SIZE = 8
H = 12


def with_ends(drawn, stream_key, low, top_value):
    spot = [jax.random.randint(jax.random.fold_in(stream_key, axis), (), 0, length) for axis, length in enumerate(drawn.shape)]
    main_axis = drawn.shape.index(max(drawn.shape))
    next_to = spot[:main_axis] + [(spot[main_axis] + 1) % drawn.shape[main_axis]] + spot[main_axis + 1:]
    return drawn.at[tuple(spot)].set(low).at[tuple(next_to)].set(top_value)


def level_of(stream_key, shape, pieces, low, top_value):
    def one(axis_at, shards_of):
        steps = jax.random.uniform(jax.random.fold_in(jax.random.fold_in(stream_key, 6), axis_at), (shards_of,), jnp.float32, low / len(pieces), top_value / len(pieces))
        return jnp.repeat(jnp.exp(steps), shape[axis_at] // shards_of).reshape((-1,) + (1,) * (len(shape) - axis_at - 1))

    gain = one(*pieces[0])
    for cut in pieces[1:]:
        gain = gain * one(*cut)
    return gain


def noise(rng, dims, width, most, shards=(), kind=jnp.bfloat16):
    drawn = width * jax.random.normal(rng, dims, jnp.float32)
    if shards:
        drawn = drawn * level_of(rng, dims, shards, -0.22, 0.18)
    return jnp.clip(drawn, -most, most).astype(kind)


def setup_inputs(seed: int = 0) -> dict:
    keys = jax.random.split(jax.random.key(seed), 8)
    return {
        "latents": noise(keys[0], (ENSEMBLE_SIZE, H, C, W), 1.0, 6.0, ((0, 8), (1, 4))),
        "filters": noise(keys[1], (K, C, C), (C * 49) ** -0.5, 0.125),
        "project": noise(keys[2], (V, C), C ** -0.5, 0.875),
        "subcell_maps": noise(keys[3], (4, V, V), V ** -0.5, 2.5),
        "verifying_truth": noise(keys[4], (4, V, H, W), 1.0, 6.0, ((2, 4), (3, 8)), jnp.float32),
        "basis_rows": with_ends(jax.random.randint(keys[5], (H, 49), 0, K + 1), jax.random.fold_in(keys[5], 1), 0, K).astype(jnp.int32),
        "step_rows": with_ends(jax.random.randint(keys[6], (H,), 1, 4), jax.random.fold_in(keys[6], 1), 1, 3).astype(jnp.int32),
    }


def latitude_cos(count):
    rows = jnp.arange(count, dtype=jnp.int32).astype(jnp.float32)
    return jnp.cos(((rows + 0.5) / count - 0.5) * jnp.pi)

def subcell_weight(first, count, total):
    rows = (first + jnp.arange(count, dtype=jnp.int32)).astype(jnp.float32)
    sub_row = jnp.array([0.0, 0.0, 1.0, 1.0], jnp.float32)
    fine = 2.0 * rows[None, :] + sub_row[:, None]
    return jnp.cos(((fine + 0.5) / (2.0 * total) - 0.5) * jnp.pi)

def softened_sign(diff):
    return diff / jnp.sqrt(diff * diff + 0.01)

def reference(latents, filters, project, subcell_maps, verifying_truth, basis_rows, step_rows):
    quad = latitude_cos(H)
    couple_factor = subcell_weight(0, H, H)
    table = jnp.concatenate([filters.astype(jnp.float32), jnp.zeros((1, C, C), jnp.float32)], 0)
    column = jnp.arange(W, dtype=jnp.int32)
    row_ids = jnp.arange(H, dtype=jnp.int32)

    def forward(latent):
        padded = jnp.pad(latent.astype(jnp.float32), ((3, 3), (0, 0), (0, 0)))
        total = jnp.zeros((H, C, W), jnp.float32)
        for tap_a in range(7):
            source = padded[tap_a:tap_a + H]
            for tap_b in range(7):
                mats = table[basis_rows[:, 7 * tap_a + tap_b]]
                offset = (tap_b - 3) * step_rows
                index = (column[None, :] + offset[:, None]) % W
                shifted = jnp.take_along_axis(source, index[:, None, :], axis=2)
                total = total + jnp.einsum('hoc,hcw->how', mats, shifted)
        filtered = total * quad[:, None, None]
        activated = jax.nn.gelu(filtered, approximate=True).astype(jnp.bfloat16)
        lowres_map = jnp.einsum('vc,hcw->vhw', project.astype(jnp.float32), activated.astype(jnp.float32)).astype(jnp.bfloat16)
        return (filtered, lowres_map)
    filtered, lowres_map = lax.map(forward, latents)
    predicted_map = jnp.einsum('svu,muhw->smvhw', subcell_maps.astype(jnp.float32), lowres_map.astype(jnp.float32), precision=lax.Precision.HIGHEST)
    predicted_map = predicted_map.astype(jnp.bfloat16).astype(jnp.float32)
    truth_error_term = softened_sign(predicted_map - verifying_truth[:, None])

    def add_couple_term(realization_number, partial_sum):
        partner_realization = lax.dynamic_index_in_dim(predicted_map, realization_number, 1, keepdims=True)
        return partial_sum + softened_sign(predicted_map - partner_realization)
    couple_spread_term = lax.fori_loop(0, ENSEMBLE_SIZE, add_couple_term, jnp.zeros_like(predicted_map))
    predicted_map_adjoint = couple_factor[:, None, None, :, None] * (truth_error_term - couple_spread_term / ENSEMBLE_SIZE)
    lowres_map_adjoint = jnp.einsum('svu,smvhw->muhw', subcell_maps.astype(jnp.float32), predicted_map_adjoint, precision=lax.Precision.HIGHEST).astype(jnp.bfloat16)

    def backward(pair):
        filtered_m, grad_coarse_m = pair
        grad_activated = jnp.einsum('vc,vhw->hcw', project.astype(jnp.float32), grad_coarse_m.astype(jnp.float32))
        pullback = jax.vjp(lambda v: jax.nn.gelu(v, approximate=True), filtered_m)[1]
        grad_filtered = pullback(grad_activated)[0].astype(jnp.bfloat16)
        padded = jnp.pad(grad_filtered.astype(jnp.float32), ((3, 3), (0, 0), (0, 0)))
        total = jnp.zeros((H, C, W), jnp.float32)
        for tap_a in range(7):
            source = padded[6 - tap_a:6 - tap_a + H]
            src_rows = jnp.clip(row_ids + 3 - tap_a, 0, H - 1)
            src_quad = quad[src_rows]
            for tap_b in range(7):
                mats = table[basis_rows[src_rows, 7 * tap_a + tap_b]]
                offset = (tap_b - 3) * step_rows[src_rows]
                index = (column[None, :] - offset[:, None]) % W
                shifted = jnp.take_along_axis(source, index[:, None, :], axis=2)
                total = total + src_quad[:, None, None] * jnp.einsum('hoc,how->hcw', mats, shifted)
        return total.astype(jnp.bfloat16)
    return lax.map(backward, (filtered, lowres_map_adjoint))
```

```python
import jax
import jax.numpy as jnp
from jax import lax
from jax.experimental import pallas as pl
from jax.experimental.pallas import tpu as pltpu
from jax.sharding import PartitionSpec as P

TAPS = 7
HALF = 3
MAX_STEP = 3


def round_up(value, unit):
    return (value + unit - 1) // unit * unit


def ring_width(width):
    return round_up(width + 4 * HALF * MAX_STEP + 2, 128)


def to_ring(block, width_p):
    width = block.shape[-1]
    extra = width_p - width
    lo = extra // 2
    hi = extra - lo
    return jnp.concatenate(
        [block, block[..., :lo], block[..., width - hi :]], axis=-1
    )


def pad_axis(block, axis, size):
    pads = [(0, 0)] * block.ndim
    pads[axis] = (0, size - block.shape[axis])
    return jnp.pad(block, pads)


def halo(block, axis_name, width):
    count = lax.axis_size(axis_name)
    forward = [(i, i + 1) for i in range(count - 1)]
    backward = [(target, source) for source, target in forward]
    low = lax.ppermute(block[block.shape[0] - width :], axis_name, forward)
    high = lax.ppermute(block[:width], axis_name, backward)
    return low, high


def latitude_rows(count, total):
    rows = jnp.arange(count, dtype=jnp.int32).astype(jnp.float32)
    return jnp.cos(((rows + 0.5) / total - 0.5) * jnp.pi)


def subcell_weight(first, count, total):
    rows = (first + jnp.arange(count, dtype=jnp.int32)).astype(jnp.float32)
    sub_row = jnp.array([0.0, 0.0, 1.0, 1.0], jnp.float32)
    fine = 2.0 * rows[None, :] + sub_row[:, None]
    return jnp.cos(((fine + 0.5) / (2.0 * total) - 0.5) * jnp.pi)


def softened_sign(diff):
    return diff / jnp.sqrt(diff * diff + 0.01)


SQRT_2_OVER_PI = 0.7978845608028654


def gelu(x):
    inner = SQRT_2_OVER_PI * (x + 0.044715 * (x * x * x))
    return x * (0.5 * (1.0 + jnp.tanh(inner)))


def gelu_grad(x):
    inner = SQRT_2_OVER_PI * (x + 0.044715 * (x * x * x))
    t = jnp.tanh(inner)
    d_inner = SQRT_2_OVER_PI * (1.0 + 3.0 * 0.044715 * (x * x))
    return 0.5 * (1.0 + t) + x * (0.5 * (1.0 - t * t)) * d_inner


def forward_kernel(shift_ref, quad_ref, prev_ref, own_ref, next_ref, w_ref, proj_ref,
                   sub_ref, filt_ref, fc_ref):
    rows, cp, _ = own_ref.shape
    ext = (
        [prev_ref[e] for e in range(HALF)]
        + [own_ref[e] for e in range(rows)]
        + [next_ref[e] for e in range(HALF)]
    )
    for i in range(rows):
        stacked = jnp.concatenate(ext[i : i + TAPS], axis=0)
        taps = jnp.dot(w_ref[i], stacked, preferred_element_type=jnp.float32)
        total = taps[HALF * cp : (HALF + 1) * cp]
        for b in range(TAPS):
            if b == HALF:
                continue
            total = total + pltpu.roll(
                taps[b * cp : (b + 1) * cp], shift_ref[i * TAPS + b], 1
            )
        filtered = total * quad_ref[i]
        filt_ref[i] = filtered
        activated = gelu(filtered).astype(jnp.bfloat16)
        coarse = jnp.dot(
            proj_ref[...], activated, preferred_element_type=jnp.float32
        ).astype(jnp.bfloat16)
        fc_ref[i] = jnp.dot(
            sub_ref[...], coarse, preferred_element_type=jnp.float32
        ).astype(jnp.bfloat16)


def grad_filtered_kernel(gc_ref, filt_ref, proj_t_ref, out_ref):
    rows = filt_ref.shape[0]
    for i in range(rows):
        grad_act = jnp.dot(proj_t_ref[...], gc_ref[i], preferred_element_type=jnp.float32)
        out_ref[i] = (grad_act * gelu_grad(filt_ref[i])).astype(jnp.bfloat16)


def backward_kernel(shift_ref, quad_ref, prev_ref, own_ref, next_ref, w_ref, out_ref):
    rows, cp, _ = own_ref.shape
    channels, width = out_ref.shape[1], out_ref.shape[2]
    ext = (
        [prev_ref[e] for e in range(HALF)]
        + [own_ref[e] for e in range(rows)]
        + [next_ref[e] for e in range(HALF)]
    )
    acc = [None] * rows
    for e in range(rows + 2 * HALF):
        a_lo = max(0, 2 * HALF - e)
        a_hi = min(TAPS - 1, rows - 1 + 2 * HALF - e)
        if a_lo > a_hi:
            continue
        source = ext[e]
        rolled = []
        for b in range(TAPS):
            if b == HALF:
                rolled.append(source)
            else:
                rolled.append(pltpu.roll(source, shift_ref[e * TAPS + b], 1))
        stacked = jnp.concatenate(rolled, axis=0)
        part = jnp.dot(
            w_ref[e, a_lo * cp : (a_hi + 1) * cp, :],
            stacked,
            preferred_element_type=jnp.float32,
        )
        scale = quad_ref[e]
        for a in range(a_lo, a_hi + 1):
            i2 = e + a - 2 * HALF
            piece = part[(a - a_lo) * cp : (a - a_lo + 1) * cp] * scale
            acc[i2] = piece if acc[i2] is None else acc[i2] + piece
    for i2 in range(rows):
        out_ref[i2] = acc[i2][:channels, :width].astype(out_ref.dtype)


def vmem():
    return pl.BlockSpec(memory_space=pltpu.VMEM)


def smem():
    return pl.BlockSpec(memory_space=pltpu.SMEM)


def on_device(latents, filters, project, subcell_maps, verifying_truth, basis_rows, step_rows):
    rows = latents.shape[1]
    channels = latents.shape[2]
    width = latents.shape[3]
    kinds = filters.shape[0]
    variables = project.shape[0]
    subcells = subcell_maps.shape[0]
    cp = round_up(channels, 16)
    vp = round_up(variables, 16)
    svp = round_up(subcells * variables, 16)
    width_p = ring_width(width)
    total_rows = rows * lax.axis_size("lat")
    first = lax.axis_index("lat") * rows

    quad_all = latitude_rows(total_rows, total_rows)
    quad = lax.dynamic_slice_in_dim(quad_all, first, rows, 0)
    couple_factor = subcell_weight(first, rows, total_rows)

    table = jnp.concatenate([filters, jnp.zeros((1,) + filters.shape[1:], filters.dtype)], 0)
    table = pad_axis(pad_axis(table, 1, cp), 2, cp)
    kind_ids = jnp.arange(kinds + 1, dtype=jnp.int32)
    taps_b = jnp.arange(TAPS, dtype=jnp.int32) - HALF

    own_basis = lax.dynamic_slice_in_dim(basis_rows, first, rows, 0).reshape(rows, TAPS, TAPS)
    own_step = lax.dynamic_slice_in_dim(step_rows, first, rows, 0)
    onehot_f = (own_basis[..., None] == kind_ids).astype(filters.dtype)
    w_fwd = jnp.einsum("iabk,koc->iboac", onehot_f, table).reshape(rows, TAPS * cp, TAPS * cp)
    shift_f = jnp.mod(-taps_b[None, :] * own_step[:, None], width_p).reshape(-1)

    pad_basis = jnp.concatenate([basis_rows[:1]] * HALF + [basis_rows] + [basis_rows[-1:]] * HALF, 0)
    pad_step = jnp.concatenate([step_rows[:1]] * HALF + [step_rows] + [step_rows[-1:]] * HALF, 0)
    pad_quad = jnp.concatenate([quad_all[:1]] * HALF + [quad_all] + [quad_all[-1:]] * HALF, 0)
    src_count = rows + 2 * HALF
    src_basis = lax.dynamic_slice_in_dim(pad_basis, first, src_count, 0).reshape(src_count, TAPS, TAPS)
    src_step = lax.dynamic_slice_in_dim(pad_step, first, src_count, 0)
    src_quad = lax.dynamic_slice_in_dim(pad_quad, first, src_count, 0)
    onehot_b = (src_basis[..., None] == kind_ids).astype(filters.dtype)
    w_bwd = jnp.einsum("eabk,koc->eacbo", onehot_b, table).reshape(
        src_count, TAPS * cp, TAPS * cp
    )
    shift_b = jnp.mod(taps_b[None, :] * src_step[:, None], width_p).reshape(-1)

    proj_p = pad_axis(pad_axis(project, 0, vp), 1, cp)
    sub_p = pad_axis(pad_axis(subcell_maps.reshape(subcells * variables, variables), 0, svp), 1, vp)

    own = to_ring(pad_axis(latents[0], 1, cp), width_p)
    low, high = halo(own, "lat", HALF)

    filtered, fc = pl.pallas_call(
        forward_kernel,
        out_shape=(
            jax.ShapeDtypeStruct((rows, cp, width_p), jnp.float32),
            jax.ShapeDtypeStruct((rows, svp, width_p), jnp.bfloat16),
        ),
        in_specs=[smem(), smem()] + [vmem()] * 6,
        out_specs=(vmem(), vmem()),
    )(shift_f, quad, low, own, high, w_fwd, proj_p, sub_p)

    forecast = fc[:, : subcells * variables, :width].reshape(rows, subcells, variables, width)
    fine_local = forecast.transpose(1, 2, 0, 3)[:, None]
    fine_owned = lax.all_to_all(fine_local, "member", split_axis=4, concat_axis=1, tiled=True)

    samples = fine_owned.astype(jnp.float32)
    members = samples.shape[1]
    truth_term = softened_sign(samples - verifying_truth[:, None])
    couple = softened_sign(samples - samples[:, 0:1])
    for n in range(1, members):
        couple = couple + softened_sign(samples - samples[:, n : n + 1])
    grad_owned = couple_factor[:, None, None, :, None] * (truth_term - couple / members)
    grad_fine = lax.all_to_all(grad_owned, "member", split_axis=1, concat_axis=4, tiled=True)
    grad_coarse = jnp.einsum(
        "svu,smvhw->muhw",
        subcell_maps.astype(jnp.float32),
        grad_fine,
        precision=lax.Precision.HIGHEST,
    )[0].astype(jnp.bfloat16)

    gc = to_ring(pad_axis(grad_coarse.transpose(1, 0, 2), 1, vp), width_p)
    proj_t = pad_axis(pad_axis(project.T, 0, cp), 1, vp)
    grad_filtered = pl.pallas_call(
        grad_filtered_kernel,
        out_shape=jax.ShapeDtypeStruct((rows, cp, width_p), jnp.bfloat16),
        in_specs=[vmem()] * 3,
        out_specs=vmem(),
    )(gc, filtered, proj_t)

    g_low, g_high = halo(grad_filtered, "lat", HALF)
    result = pl.pallas_call(
        backward_kernel,
        out_shape=jax.ShapeDtypeStruct((rows, channels, width), jnp.bfloat16),
        in_specs=[smem(), smem()] + [vmem()] * 4,
        out_specs=vmem(),
    )(shift_b, src_quad, g_low, grad_filtered, g_high, w_bwd)
    return result[None]


def solution(mesh):
    placed = (
        P("member", "lat", None, None),
        P(),
        P(),
        P(),
        P(None, None, "lat", "member"),
        P(),
        P(),
    )
    return jax.shard_map(
        on_device,
        mesh=mesh,
        in_specs=placed,
        out_specs=P("member", "lat", None, None),
        check_vma=False,
    )
```

```python
import jax
import jax.numpy as jnp
from jax import lax
from jax.experimental import pallas as pl
from jax.experimental.pallas import tpu as pltpu
from jax.sharding import PartitionSpec as P

TAPS = 7
HALF = 3
MAX_STEP = 3


def round_up(value, unit):
    return (value + unit - 1) // unit * unit


def ring_width(width):
    return round_up(width + 4 * HALF * MAX_STEP + 2, 128)


def to_ring(block, width_p):
    width = block.shape[-1]
    extra = width_p - width
    lo = extra // 2
    hi = extra - lo
    return jnp.concatenate(
        [block, block[..., :lo], block[..., width - hi :]], axis=-1
    )


def pad_axis(block, axis, size):
    pads = [(0, 0)] * block.ndim
    pads[axis] = (0, size - block.shape[axis])
    return jnp.pad(block, pads)


def halo(block, axis_name, width):
    count = lax.axis_size(axis_name)
    forward = [(i, i + 1) for i in range(count - 1)]
    backward = [(target, source) for source, target in forward]
    low = lax.ppermute(block[block.shape[0] - width :], axis_name, forward)
    high = lax.ppermute(block[:width], axis_name, backward)
    return low, high


def latitude_rows(count, total):
    rows = jnp.arange(count, dtype=jnp.int32).astype(jnp.float32)
    return jnp.cos(((rows + 0.5) / total - 0.5) * jnp.pi)


def subcell_weight(first, count, total):
    rows = (first + jnp.arange(count, dtype=jnp.int32)).astype(jnp.float32)
    sub_row = jnp.array([0.0, 0.0, 1.0, 1.0], jnp.float32)
    fine = 2.0 * rows[None, :] + sub_row[:, None]
    return jnp.cos(((fine + 0.5) / (2.0 * total) - 0.5) * jnp.pi)


def softened_sign(diff):
    return diff / jnp.sqrt(diff * diff + 0.01)


SQRT_2_OVER_PI = 0.7978845608028654


def gelu(x):
    inner = SQRT_2_OVER_PI * (x + 0.044715 * (x * x * x))
    return x * (0.5 * (1.0 + jnp.tanh(inner)))


def gelu_grad(x):
    inner = SQRT_2_OVER_PI * (x + 0.044715 * (x * x * x))
    t = jnp.tanh(inner)
    d_inner = SQRT_2_OVER_PI * (1.0 + 3.0 * 0.044715 * (x * x))
    return 0.5 * (1.0 + t) + x * (0.5 * (1.0 - t * t)) * d_inner


def forward_kernel(basis_ref, step_ref, quad_ref, prev_ref, own_ref, next_ref, table_ref,
                   proj_ref, sub_ref, filt_ref, fc_ref):
    rows, cp, width_p = own_ref.shape
    first = lax.axis_index("lat") * rows
    ext = (
        [prev_ref[e] for e in range(HALF)]
        + [own_ref[e] for e in range(rows)]
        + [next_ref[e] for e in range(HALF)]
    )
    for i in range(rows):
        g = first + i
        step = step_ref[g]
        weights = jnp.concatenate(
            [
                jnp.concatenate(
                    [table_ref[0, basis_ref[g * TAPS * TAPS + a * TAPS + b]] for a in range(TAPS)],
                    axis=1,
                )
                for b in range(TAPS)
            ],
            axis=0,
        )
        stacked = jnp.concatenate(ext[i : i + TAPS], axis=0)
        taps = jnp.dot(weights, stacked, preferred_element_type=jnp.float32)
        total = taps[HALF * cp : (HALF + 1) * cp]
        for b in range(TAPS):
            if b == HALF:
                continue
            shift = lax.rem((HALF - b) * step + width_p, width_p)
            total = total + pltpu.roll(taps[b * cp : (b + 1) * cp], shift, 1)
        filtered = total * quad_ref[g]
        filt_ref[i] = filtered
        activated = gelu(filtered).astype(jnp.bfloat16)
        coarse = jnp.dot(
            proj_ref[...], activated, preferred_element_type=jnp.float32
        ).astype(jnp.bfloat16)
        fc_ref[i] = jnp.dot(
            sub_ref[...], coarse, preferred_element_type=jnp.float32
        ).astype(jnp.bfloat16)


def grad_filtered_kernel(gc_ref, filt_ref, proj_t_ref, out_ref):
    rows = filt_ref.shape[0]
    for i in range(rows):
        grad_act = jnp.dot(proj_t_ref[...], gc_ref[i], preferred_element_type=jnp.float32)
        out_ref[i] = (grad_act * gelu_grad(filt_ref[i])).astype(jnp.bfloat16)


def backward_kernel(basis_ref, step_ref, quad_ref, prev_ref, own_ref, next_ref, table_ref,
                    out_ref):
    rows, cp, width_p = own_ref.shape
    channels, width = out_ref.shape[1], out_ref.shape[2]
    total_rows = step_ref.shape[0]
    first = lax.axis_index("lat") * rows
    ext = (
        [prev_ref[e] for e in range(HALF)]
        + [own_ref[e] for e in range(rows)]
        + [next_ref[e] for e in range(HALF)]
    )
    acc = [None] * rows
    for e in range(rows + 2 * HALF):
        a_lo = max(0, 2 * HALF - e)
        a_hi = min(TAPS - 1, rows - 1 + 2 * HALF - e)
        if a_lo > a_hi:
            continue
        g = jnp.clip(first - HALF + e, 0, total_rows - 1)
        step = step_ref[g]
        weights = jnp.concatenate(
            [
                jnp.concatenate(
                    [table_ref[1, basis_ref[g * TAPS * TAPS + a * TAPS + b]] for b in range(TAPS)],
                    axis=1,
                )
                for a in range(a_lo, a_hi + 1)
            ],
            axis=0,
        )
        source = ext[e]
        rolled = []
        for b in range(TAPS):
            if b == HALF:
                rolled.append(source)
            else:
                shift = lax.rem((b - HALF) * step + width_p, width_p)
                rolled.append(pltpu.roll(source, shift, 1))
        stacked = jnp.concatenate(rolled, axis=0)
        part = jnp.dot(weights, stacked, preferred_element_type=jnp.float32)
        scale = quad_ref[g]
        for a in range(a_lo, a_hi + 1):
            i2 = e + a - 2 * HALF
            piece = part[(a - a_lo) * cp : (a - a_lo + 1) * cp] * scale
            acc[i2] = piece if acc[i2] is None else acc[i2] + piece
    for i2 in range(rows):
        out_ref[i2] = acc[i2][:channels, :width].astype(out_ref.dtype)


def vmem():
    return pl.BlockSpec(memory_space=pltpu.VMEM)


def smem():
    return pl.BlockSpec(memory_space=pltpu.SMEM)


def on_device(latents, filters, project, subcell_maps, verifying_truth, basis_rows, step_rows):
    rows = latents.shape[1]
    channels = latents.shape[2]
    width = latents.shape[3]
    variables = project.shape[0]
    subcells = subcell_maps.shape[0]
    cp = round_up(channels, 16)
    vp = round_up(variables, 16)
    svp = round_up(subcells * variables, 16)
    width_p = ring_width(width)
    total_rows = rows * lax.axis_size("lat")
    first = lax.axis_index("lat") * rows

    quad_all = latitude_rows(total_rows, total_rows)
    couple_factor = subcell_weight(first, rows, total_rows)

    table = jnp.concatenate([filters, jnp.zeros((1,) + filters.shape[1:], filters.dtype)], 0)
    table = pad_axis(pad_axis(table, 1, cp), 2, cp)
    tables = jnp.stack([table, table.transpose(0, 2, 1)])
    basis_flat = basis_rows.reshape(-1)

    proj_p = pad_axis(pad_axis(project, 0, vp), 1, cp)
    sub_p = pad_axis(pad_axis(subcell_maps.reshape(subcells * variables, variables), 0, svp), 1, vp)

    own = to_ring(pad_axis(latents[0], 1, cp), width_p)
    low, high = halo(own, "lat", HALF)

    filtered, fc = pl.pallas_call(
        forward_kernel,
        out_shape=(
            jax.ShapeDtypeStruct((rows, cp, width_p), jnp.float32),
            jax.ShapeDtypeStruct((rows, svp, width_p), jnp.bfloat16),
        ),
        in_specs=[smem(), smem(), smem()] + [vmem()] * 6,
        out_specs=(vmem(), vmem()),
    )(basis_flat, step_rows, quad_all, low, own, high, tables, proj_p, sub_p)

    forecast = fc[:, : subcells * variables, :width].reshape(rows, subcells, variables, width)
    fine_local = forecast.transpose(1, 2, 0, 3)[:, None]
    fine_owned = lax.all_to_all(fine_local, "member", split_axis=4, concat_axis=1, tiled=True)

    samples = fine_owned.astype(jnp.float32)
    members = samples.shape[1]
    truth_term = softened_sign(samples - verifying_truth[:, None])
    couple = softened_sign(samples - samples[:, 0:1])
    for n in range(1, members):
        couple = couple + softened_sign(samples - samples[:, n : n + 1])
    grad_owned = couple_factor[:, None, None, :, None] * (truth_term - couple / members)
    grad_fine = lax.all_to_all(grad_owned, "member", split_axis=1, concat_axis=4, tiled=True)
    grad_coarse = jnp.einsum(
        "svu,smvhw->muhw",
        subcell_maps.astype(jnp.float32),
        grad_fine,
        precision=lax.Precision.HIGHEST,
    )[0].astype(jnp.bfloat16)

    gc = to_ring(pad_axis(grad_coarse.transpose(1, 0, 2), 1, vp), width_p)
    proj_t = pad_axis(pad_axis(project.T, 0, cp), 1, vp)
    grad_filtered = pl.pallas_call(
        grad_filtered_kernel,
        out_shape=jax.ShapeDtypeStruct((rows, cp, width_p), jnp.bfloat16),
        in_specs=[vmem()] * 3,
        out_specs=vmem(),
    )(gc, filtered, proj_t)

    g_low, g_high = halo(grad_filtered, "lat", HALF)
    result = pl.pallas_call(
        backward_kernel,
        out_shape=jax.ShapeDtypeStruct((rows, channels, width), jnp.bfloat16),
        in_specs=[smem(), smem(), smem()] + [vmem()] * 4,
        out_specs=vmem(),
    )(basis_flat, step_rows, quad_all, g_low, grad_filtered, g_high, tables)
    return result[None]


def solution(mesh):
    placed = (
        P("member", "lat", None, None),
        P(),
        P(),
        P(),
        P(None, None, "lat", "member"),
        P(),
        P(),
    )
    return jax.shard_map(
        on_device,
        mesh=mesh,
        in_specs=placed,
        out_specs=P("member", "lat", None, None),
        check_vma=False,
    )
```

```python
import jax
import jax.numpy as jnp
from jax import lax
from jax.experimental import pallas as pl
from jax.experimental.pallas import tpu as pltpu
from jax.sharding import PartitionSpec as P

TAPS = 7
HALF = 3
MAX_STEP = 3


def round_up(value, unit):
    return (value + unit - 1) // unit * unit


def ring_width(width):
    return round_up(width + 4 * HALF * MAX_STEP + 2, 128)


def to_ring(block, width_p):
    width = block.shape[-1]
    extra = width_p - width
    lo = extra // 2
    hi = extra - lo
    return jnp.concatenate(
        [block, block[..., :lo], block[..., width - hi :]], axis=-1
    )


def pad_axis(block, axis, size):
    pads = [(0, 0)] * block.ndim
    pads[axis] = (0, size - block.shape[axis])
    return jnp.pad(block, pads)


def halo(block, axis_name, width):
    count = lax.axis_size(axis_name)
    forward = [(i, i + 1) for i in range(count - 1)]
    backward = [(target, source) for source, target in forward]
    low = lax.ppermute(block[block.shape[0] - width :], axis_name, forward)
    high = lax.ppermute(block[:width], axis_name, backward)
    return low, high


def latitude_rows(count, total):
    rows = jnp.arange(count, dtype=jnp.int32).astype(jnp.float32)
    return jnp.cos(((rows + 0.5) / total - 0.5) * jnp.pi)


def subcell_weight(first, count, total):
    rows = (first + jnp.arange(count, dtype=jnp.int32)).astype(jnp.float32)
    sub_row = jnp.array([0.0, 0.0, 1.0, 1.0], jnp.float32)
    fine = 2.0 * rows[None, :] + sub_row[:, None]
    return jnp.cos(((fine + 0.5) / (2.0 * total) - 0.5) * jnp.pi)


def softened_sign(diff):
    return diff / jnp.sqrt(diff * diff + 0.01)


SQRT_2_OVER_PI = 0.7978845608028654


def gelu(x):
    inner = SQRT_2_OVER_PI * (x + 0.044715 * (x * x * x))
    return x * (0.5 * (1.0 + jnp.tanh(inner)))


def gelu_grad(x):
    inner = SQRT_2_OVER_PI * (x + 0.044715 * (x * x * x))
    t = jnp.tanh(inner)
    d_inner = SQRT_2_OVER_PI * (1.0 + 3.0 * 0.044715 * (x * x))
    return 0.5 * (1.0 + t) + x * (0.5 * (1.0 - t * t)) * d_inner


def forward_kernel(basis_ref, step_ref, quad_ref, prev_ref, own_ref, next_ref, table_ref,
                   proj_ref, sub_ref, filt_ref, fc_ref):
    rows, cp, width_p = own_ref.shape
    first = lax.axis_index("lat") * rows
    ext = (
        [prev_ref[e] for e in range(HALF)]
        + [own_ref[e] for e in range(rows)]
        + [next_ref[e] for e in range(HALF)]
    )
    for i in range(rows):
        g = first + i
        step = step_ref[g]
        weights = jnp.concatenate(
            [
                jnp.concatenate(
                    [table_ref[0, basis_ref[g * TAPS * TAPS + a * TAPS + b]] for a in range(TAPS)],
                    axis=1,
                )
                for b in range(TAPS)
            ],
            axis=0,
        )
        stacked = jnp.concatenate(ext[i : i + TAPS], axis=0)
        taps = jnp.dot(weights, stacked, preferred_element_type=jnp.float32)
        total = taps[HALF * cp : (HALF + 1) * cp]
        for b in range(TAPS):
            if b == HALF:
                continue
            shift = lax.rem((HALF - b) * step + width_p, width_p)
            total = total + pltpu.roll(taps[b * cp : (b + 1) * cp], shift, 1)
        filtered = total * quad_ref[g]
        filt_ref[i] = filtered
        activated = gelu(filtered).astype(jnp.bfloat16)
        coarse = jnp.dot(
            proj_ref[...], activated, preferred_element_type=jnp.float32
        ).astype(jnp.bfloat16)
        fc_ref[i] = jnp.dot(
            sub_ref[...], coarse, preferred_element_type=jnp.float32
        ).astype(jnp.bfloat16)


def score_kernel(sub_ref, weight_ref, fc_ref, truth_ref, filt_ref, proj_t_ref, out_ref):
    members, rows, cells, width_p = fc_ref.shape
    variables = sub_ref.shape[0] // cells
    subcells = cells // variables
    vp = proj_t_ref.shape[1]
    total_rows = weight_ref.shape[0] // subcells
    me = lax.axis_index("member")
    first = lax.axis_index("lat") * rows
    cell_sub = lax.broadcasted_iota(jnp.int32, (cells, 1), 0) // variables
    for i in range(rows):
        g = first + i
        mine = fc_ref[me, i].astype(jnp.float32)
        spread = None
        for n in range(members):
            term = softened_sign(mine - fc_ref[n, i].astype(jnp.float32))
            spread = term if spread is None else spread + term
        scale = jnp.zeros((cells, 1), jnp.float32)
        for s in range(subcells):
            scale = jnp.where(cell_sub == s, weight_ref[s * total_rows + g], scale)
        grad = scale * (softened_sign(mine - truth_ref[i]) - spread / members)
        coarse = []
        for u in range(vp):
            if u >= variables:
                coarse.append(jnp.zeros((1, width_p), jnp.float32))
                continue
            acc = None
            for r in range(cells):
                term = sub_ref[r * variables + u] * grad[r : r + 1]
                acc = term if acc is None else acc + term
            coarse.append(acc)
        grad_coarse = jnp.concatenate(coarse, axis=0).astype(jnp.bfloat16)
        grad_act = jnp.dot(proj_t_ref[...], grad_coarse, preferred_element_type=jnp.float32)
        out_ref[i] = (grad_act * gelu_grad(filt_ref[i])).astype(jnp.bfloat16)


def backward_kernel(basis_ref, step_ref, quad_ref, prev_ref, own_ref, next_ref, table_ref,
                    out_ref):
    rows, cp, width_p = own_ref.shape
    channels, width = out_ref.shape[1], out_ref.shape[2]
    total_rows = step_ref.shape[0]
    first = lax.axis_index("lat") * rows
    ext = (
        [prev_ref[e] for e in range(HALF)]
        + [own_ref[e] for e in range(rows)]
        + [next_ref[e] for e in range(HALF)]
    )
    acc = [None] * rows
    for e in range(rows + 2 * HALF):
        a_lo = max(0, 2 * HALF - e)
        a_hi = min(TAPS - 1, rows - 1 + 2 * HALF - e)
        if a_lo > a_hi:
            continue
        g = jnp.clip(first - HALF + e, 0, total_rows - 1)
        step = step_ref[g]
        weights = jnp.concatenate(
            [
                jnp.concatenate(
                    [table_ref[1, basis_ref[g * TAPS * TAPS + a * TAPS + b]] for b in range(TAPS)],
                    axis=1,
                )
                for a in range(a_lo, a_hi + 1)
            ],
            axis=0,
        )
        source = ext[e]
        rolled = []
        for b in range(TAPS):
            if b == HALF:
                rolled.append(source)
            else:
                shift = lax.rem((b - HALF) * step + width_p, width_p)
                rolled.append(pltpu.roll(source, shift, 1))
        stacked = jnp.concatenate(rolled, axis=0)
        part = jnp.dot(weights, stacked, preferred_element_type=jnp.float32)
        scale = quad_ref[g]
        for a in range(a_lo, a_hi + 1):
            i2 = e + a - 2 * HALF
            piece = part[(a - a_lo) * cp : (a - a_lo + 1) * cp] * scale
            acc[i2] = piece if acc[i2] is None else acc[i2] + piece
    for i2 in range(rows):
        out_ref[i2] = acc[i2][:channels, :width].astype(out_ref.dtype)


def vmem():
    return pl.BlockSpec(memory_space=pltpu.VMEM)


def smem():
    return pl.BlockSpec(memory_space=pltpu.SMEM)


def on_device(latents, filters, project, subcell_maps, verifying_truth, basis_rows, step_rows):
    rows = latents.shape[1]
    channels = latents.shape[2]
    width = latents.shape[3]
    variables = project.shape[0]
    subcells = subcell_maps.shape[0]
    cp = round_up(channels, 16)
    vp = round_up(variables, 16)
    svp = subcells * variables
    width_p = ring_width(width)
    total_rows = rows * lax.axis_size("lat")
    first = lax.axis_index("lat") * rows

    quad_all = latitude_rows(total_rows, total_rows)
    weight_all = subcell_weight(0, total_rows, total_rows).reshape(-1)
    sub_flat = subcell_maps.astype(jnp.float32).reshape(-1)
    truth_all = lax.all_gather(verifying_truth, "member", axis=3, tiled=True)
    truth_ring = to_ring(
        truth_all.reshape(subcells * variables, rows, width).transpose(1, 0, 2), width_p
    )

    table = jnp.concatenate([filters, jnp.zeros((1,) + filters.shape[1:], filters.dtype)], 0)
    table = pad_axis(pad_axis(table, 1, cp), 2, cp)
    tables = jnp.stack([table, table.transpose(0, 2, 1)])
    basis_flat = basis_rows.reshape(-1)

    proj_p = pad_axis(pad_axis(project, 0, vp), 1, cp)
    sub_p = pad_axis(pad_axis(subcell_maps.reshape(subcells * variables, variables), 0, svp), 1, vp)

    own = to_ring(pad_axis(latents[0], 1, cp), width_p)
    low, high = halo(own, "lat", HALF)

    filtered, fc = pl.pallas_call(
        forward_kernel,
        out_shape=(
            jax.ShapeDtypeStruct((rows, cp, width_p), jnp.float32),
            jax.ShapeDtypeStruct((rows, svp, width_p), jnp.bfloat16),
        ),
        in_specs=[smem(), smem(), smem()] + [vmem()] * 6,
        out_specs=(vmem(), vmem()),
    )(basis_flat, step_rows, quad_all, low, own, high, tables, proj_p, sub_p)

    gathered = lax.all_gather(fc, "member", axis=0, tiled=False)
    proj_t = pad_axis(pad_axis(project.T, 0, cp), 1, vp)
    grad_filtered = pl.pallas_call(
        score_kernel,
        out_shape=jax.ShapeDtypeStruct((rows, cp, width_p), jnp.bfloat16),
        in_specs=[smem(), smem()] + [vmem()] * 4,
        out_specs=vmem(),
    )(sub_flat, weight_all, gathered, truth_ring, filtered, proj_t)

    g_low, g_high = halo(grad_filtered, "lat", HALF)
    result = pl.pallas_call(
        backward_kernel,
        out_shape=jax.ShapeDtypeStruct((rows, channels, width), jnp.bfloat16),
        in_specs=[smem(), smem(), smem()] + [vmem()] * 4,
        out_specs=vmem(),
    )(basis_flat, step_rows, quad_all, g_low, grad_filtered, g_high, tables)
    return result[None]


def solution(mesh):
    placed = (
        P("member", "lat", None, None),
        P(),
        P(),
        P(),
        P(None, None, "lat", "member"),
        P(),
        P(),
    )
    return jax.shard_map(
        on_device,
        mesh=mesh,
        in_specs=placed,
        out_specs=P("member", "lat", None, None),
        check_vma=False,
    )
```

```python
import jax
import jax.numpy as jnp
from jax import lax
from jax.experimental import pallas as pl
from jax.experimental.pallas import tpu as pltpu
from jax.sharding import PartitionSpec as P

TAPS = 7
HALF = 3
MAX_STEP = 3


def round_up(value, unit):
    return (value + unit - 1) // unit * unit


def ring_width(width):
    return round_up(width + 4 * HALF * MAX_STEP + 2, 128)


def to_ring(block, width_p):
    width = block.shape[-1]
    extra = width_p - width
    lo = extra // 2
    hi = extra - lo
    return jnp.concatenate(
        [block, block[..., :lo], block[..., width - hi :]], axis=-1
    )


def pad_axis(block, axis, size):
    pads = [(0, 0)] * block.ndim
    pads[axis] = (0, size - block.shape[axis])
    return jnp.pad(block, pads)


def halo(block, axis_name, width):
    count = lax.axis_size(axis_name)
    forward = [(i, i + 1) for i in range(count - 1)]
    backward = [(target, source) for source, target in forward]
    low = lax.ppermute(block[block.shape[0] - width :], axis_name, forward)
    high = lax.ppermute(block[:width], axis_name, backward)
    return low, high


def latitude_rows(count, total):
    rows = jnp.arange(count, dtype=jnp.int32).astype(jnp.float32)
    return jnp.cos(((rows + 0.5) / total - 0.5) * jnp.pi)


def subcell_weight(first, count, total):
    rows = (first + jnp.arange(count, dtype=jnp.int32)).astype(jnp.float32)
    sub_row = jnp.array([0.0, 0.0, 1.0, 1.0], jnp.float32)
    fine = 2.0 * rows[None, :] + sub_row[:, None]
    return jnp.cos(((fine + 0.5) / (2.0 * total) - 0.5) * jnp.pi)


def softened_sign(diff):
    return diff / jnp.sqrt(diff * diff + 0.01)


SQRT_2_OVER_PI = 0.7978845608028654


def gelu(x):
    inner = SQRT_2_OVER_PI * (x + 0.044715 * (x * x * x))
    return x * (0.5 * (1.0 + jnp.tanh(inner)))


def gelu_grad(x):
    inner = SQRT_2_OVER_PI * (x + 0.044715 * (x * x * x))
    t = jnp.tanh(inner)
    d_inner = SQRT_2_OVER_PI * (1.0 + 3.0 * 0.044715 * (x * x))
    return 0.5 * (1.0 + t) + x * (0.5 * (1.0 - t * t)) * d_inner


def forward_kernel(basis_ref, step_ref, quad_ref, prev_ref, own_ref, next_ref, table_ref,
                   proj_ref, sub_ref, filt_ref, fc_ref):
    rows, cp, width_p = own_ref.shape
    first = lax.axis_index("lat") * rows
    ext = (
        [prev_ref[e] for e in range(HALF)]
        + [own_ref[e] for e in range(rows)]
        + [next_ref[e] for e in range(HALF)]
    )
    for i in range(rows):
        g = first + i
        step = step_ref[g]
        weights = jnp.concatenate(
            [
                jnp.concatenate(
                    [table_ref[0, basis_ref[g * TAPS * TAPS + a * TAPS + b]] for a in range(TAPS)],
                    axis=1,
                )
                for b in range(TAPS)
            ],
            axis=0,
        )
        stacked = jnp.concatenate(ext[i : i + TAPS], axis=0)
        taps = jnp.dot(weights, stacked, preferred_element_type=jnp.float32)
        total = taps[HALF * cp : (HALF + 1) * cp]
        for b in range(TAPS):
            if b == HALF:
                continue
            shift = lax.rem((HALF - b) * step + width_p, width_p)
            total = total + pltpu.roll(taps[b * cp : (b + 1) * cp], shift, 1)
        filtered = total * quad_ref[g]
        filt_ref[i] = filtered
        activated = gelu(filtered).astype(jnp.bfloat16)
        coarse = jnp.dot(
            proj_ref[...], activated, preferred_element_type=jnp.float32
        ).astype(jnp.bfloat16)
        forecast = jnp.dot(
            sub_ref[...], coarse, preferred_element_type=jnp.float32
        ).astype(jnp.bfloat16)
        blocks, block = fc_ref.shape[0], fc_ref.shape[3]
        for q in range(blocks):
            fc_ref[q, i] = forecast[:, q * block : (q + 1) * block]


def score_kernel(sub_ref, weight_ref, fc_ref, truth_ref, out_ref):
    members, rows, cells, block = fc_ref.shape
    vp = out_ref.shape[2]
    variables = sub_ref.shape[0] // cells
    subcells = cells // variables
    total_rows = weight_ref.shape[0] // subcells
    first = lax.axis_index("lat") * rows
    cell_sub = lax.broadcasted_iota(jnp.int32, (cells, 1), 0) // variables
    for i in range(rows):
        g = first + i
        scale = jnp.zeros((cells, 1), jnp.float32)
        for s in range(subcells):
            scale = jnp.where(cell_sub == s, weight_ref[s * total_rows + g], scale)
        truth = truth_ref[i]
        values = [fc_ref[n, i].astype(jnp.float32) for n in range(members)]
        spread = [jnp.zeros((cells, block), jnp.float32) for _ in range(members)]
        for m in range(members):
            for n in range(m + 1, members):
                term = softened_sign(values[m] - values[n])
                spread[m] = spread[m] + term
                spread[n] = spread[n] - term
        for m in range(members):
            grad = scale * (softened_sign(values[m] - truth) - spread[m] / members)
            coarse = []
            for u in range(vp):
                if u >= variables:
                    coarse.append(jnp.zeros((1, block), jnp.float32))
                    continue
                acc = None
                for r in range(cells):
                    term = sub_ref[r * variables + u] * grad[r : r + 1]
                    acc = term if acc is None else acc + term
                coarse.append(acc)
            out_ref[m, i] = jnp.concatenate(coarse, axis=0).astype(out_ref.dtype)


def grad_filtered_kernel(gc_ref, filt_ref, proj_t_ref, out_ref):
    blocks, rows = gc_ref.shape[0], gc_ref.shape[1]
    width_p = filt_ref.shape[2]
    for i in range(rows):
        row = jnp.concatenate([gc_ref[q, i] for q in range(blocks)], axis=1)
        width = row.shape[1]
        extra = width_p - width
        lo = extra // 2
        hi = extra - lo
        ring = jnp.concatenate([row, row[:, :lo], row[:, width - hi :]], axis=1)
        grad_act = jnp.dot(proj_t_ref[...], ring, preferred_element_type=jnp.float32)
        out_ref[i] = (grad_act * gelu_grad(filt_ref[i])).astype(jnp.bfloat16)


def backward_kernel(basis_ref, step_ref, quad_ref, prev_ref, own_ref, next_ref, table_ref,
                    out_ref):
    rows, cp, width_p = own_ref.shape
    channels, width = out_ref.shape[1], out_ref.shape[2]
    total_rows = step_ref.shape[0]
    first = lax.axis_index("lat") * rows
    ext = (
        [prev_ref[e] for e in range(HALF)]
        + [own_ref[e] for e in range(rows)]
        + [next_ref[e] for e in range(HALF)]
    )
    acc = [None] * rows
    for e in range(rows + 2 * HALF):
        a_lo = max(0, 2 * HALF - e)
        a_hi = min(TAPS - 1, rows - 1 + 2 * HALF - e)
        if a_lo > a_hi:
            continue
        g = jnp.clip(first - HALF + e, 0, total_rows - 1)
        step = step_ref[g]
        weights = jnp.concatenate(
            [
                jnp.concatenate(
                    [table_ref[1, basis_ref[g * TAPS * TAPS + a * TAPS + b]] for b in range(TAPS)],
                    axis=1,
                )
                for a in range(a_lo, a_hi + 1)
            ],
            axis=0,
        )
        source = ext[e]
        rolled = []
        for b in range(TAPS):
            if b == HALF:
                rolled.append(source)
            else:
                shift = lax.rem((b - HALF) * step + width_p, width_p)
                rolled.append(pltpu.roll(source, shift, 1))
        stacked = jnp.concatenate(rolled, axis=0)
        part = jnp.dot(weights, stacked, preferred_element_type=jnp.float32)
        scale = quad_ref[g]
        for a in range(a_lo, a_hi + 1):
            i2 = e + a - 2 * HALF
            piece = part[(a - a_lo) * cp : (a - a_lo + 1) * cp] * scale
            acc[i2] = piece if acc[i2] is None else acc[i2] + piece
    for i2 in range(rows):
        out_ref[i2] = acc[i2][:channels, :width].astype(out_ref.dtype)


def vmem():
    return pl.BlockSpec(memory_space=pltpu.VMEM)


def smem():
    return pl.BlockSpec(memory_space=pltpu.SMEM)


def on_device(latents, filters, project, subcell_maps, verifying_truth, basis_rows, step_rows):
    rows = latents.shape[1]
    channels = latents.shape[2]
    width = latents.shape[3]
    variables = project.shape[0]
    subcells = subcell_maps.shape[0]
    cp = round_up(channels, 16)
    vp = round_up(variables, 16)
    svp = subcells * variables
    width_p = ring_width(width)
    total_rows = rows * lax.axis_size("lat")
    first = lax.axis_index("lat") * rows

    quad_all = latitude_rows(total_rows, total_rows)
    weight_all = subcell_weight(0, total_rows, total_rows).reshape(-1)
    sub_flat = subcell_maps.astype(jnp.float32).reshape(-1)
    blocks = lax.axis_size("member")
    block = width // blocks
    truth = verifying_truth.reshape(subcells * variables, rows, block).transpose(1, 0, 2)

    table = jnp.concatenate([filters, jnp.zeros((1,) + filters.shape[1:], filters.dtype)], 0)
    table = pad_axis(pad_axis(table, 1, cp), 2, cp)
    tables = jnp.stack([table, table.transpose(0, 2, 1)])
    basis_flat = basis_rows.reshape(-1)

    proj_p = pad_axis(pad_axis(project, 0, vp), 1, cp)
    sub_p = pad_axis(pad_axis(subcell_maps.reshape(subcells * variables, variables), 0, svp), 1, vp)

    own = to_ring(pad_axis(latents[0], 1, cp), width_p)
    low, high = halo(own, "lat", HALF)

    filtered, fc = pl.pallas_call(
        forward_kernel,
        out_shape=(
            jax.ShapeDtypeStruct((rows, cp, width_p), jnp.float32),
            jax.ShapeDtypeStruct((blocks, rows, svp, block), jnp.bfloat16),
        ),
        in_specs=[smem(), smem(), smem()] + [vmem()] * 6,
        out_specs=(vmem(), vmem()),
    )(basis_flat, step_rows, quad_all, low, own, high, tables, proj_p, sub_p)

    fc_owned = lax.all_to_all(fc, "member", split_axis=0, concat_axis=0, tiled=True)
    gc_owned = pl.pallas_call(
        score_kernel,
        out_shape=jax.ShapeDtypeStruct((blocks, rows, vp, block), jnp.bfloat16),
        in_specs=[smem(), smem()] + [vmem()] * 2,
        out_specs=vmem(),
    )(sub_flat, weight_all, fc_owned, truth)
    gc_home = lax.all_to_all(gc_owned, "member", split_axis=0, concat_axis=0, tiled=True)
    proj_t = pad_axis(pad_axis(project.T, 0, cp), 1, vp)
    grad_filtered = pl.pallas_call(
        grad_filtered_kernel,
        out_shape=jax.ShapeDtypeStruct((rows, cp, width_p), jnp.bfloat16),
        in_specs=[vmem()] * 3,
        out_specs=vmem(),
    )(gc_home, filtered, proj_t)

    g_low, g_high = halo(grad_filtered, "lat", HALF)
    result = pl.pallas_call(
        backward_kernel,
        out_shape=jax.ShapeDtypeStruct((rows, channels, width), jnp.bfloat16),
        in_specs=[smem(), smem(), smem()] + [vmem()] * 4,
        out_specs=vmem(),
    )(basis_flat, step_rows, quad_all, g_low, grad_filtered, g_high, tables)
    return result[None]


def solution(mesh):
    placed = (
        P("member", "lat", None, None),
        P(),
        P(),
        P(),
        P(None, None, "lat", "member"),
        P(),
        P(),
    )
    return jax.shard_map(
        on_device,
        mesh=mesh,
        in_specs=placed,
        out_specs=P("member", "lat", None, None),
        check_vma=False,
    )
```

```python
import jax
import jax.numpy as jnp
from jax import lax
from jax.experimental import pallas as pl
from jax.experimental.pallas import tpu as pltpu
from jax.sharding import PartitionSpec as P

TAPS = 7
HALF = 3
MAX_STEP = 3


def round_up(value, unit):
    return (value + unit - 1) // unit * unit


def ring_width(width):
    return round_up(width + 4 * HALF * MAX_STEP + 2, 128)


def to_ring(block, width_p):
    width = block.shape[-1]
    extra = width_p - width
    lo = extra // 2
    hi = extra - lo
    return jnp.concatenate(
        [block, block[..., :lo], block[..., width - hi :]], axis=-1
    )


def pad_axis(block, axis, size):
    pads = [(0, 0)] * block.ndim
    pads[axis] = (0, size - block.shape[axis])
    return jnp.pad(block, pads)


def halo(block, axis_name, width, axis=0):
    count = lax.axis_size(axis_name)
    forward = [(i, i + 1) for i in range(count - 1)]
    backward = [(target, source) for source, target in forward]
    size = block.shape[axis]
    low = lax.ppermute(lax.slice_in_dim(block, size - width, size, axis=axis), axis_name, forward)
    high = lax.ppermute(lax.slice_in_dim(block, 0, width, axis=axis), axis_name, backward)
    return low, high


def latitude_rows(count, total):
    rows = jnp.arange(count, dtype=jnp.int32).astype(jnp.float32)
    return jnp.cos(((rows + 0.5) / total - 0.5) * jnp.pi)


def subcell_weight(first, count, total):
    rows = (first + jnp.arange(count, dtype=jnp.int32)).astype(jnp.float32)
    sub_row = jnp.array([0.0, 0.0, 1.0, 1.0], jnp.float32)
    fine = 2.0 * rows[None, :] + sub_row[:, None]
    return jnp.cos(((fine + 0.5) / (2.0 * total) - 0.5) * jnp.pi)


def softened_sign(diff):
    return diff / jnp.sqrt(diff * diff + 0.01)


SQRT_2_OVER_PI = 0.7978845608028654


def gelu(x):
    inner = SQRT_2_OVER_PI * (x + 0.044715 * (x * x * x))
    return x * (0.5 * (1.0 + jnp.tanh(inner)))


def gelu_grad(x):
    inner = SQRT_2_OVER_PI * (x + 0.044715 * (x * x * x))
    t = jnp.tanh(inner)
    d_inner = SQRT_2_OVER_PI * (1.0 + 3.0 * 0.044715 * (x * x))
    return 0.5 * (1.0 + t) + x * (0.5 * (1.0 - t * t)) * d_inner


def forward_kernel(basis_ref, step_ref, quad_ref, prev_ref, own_ref, next_ref, table_ref,
                   proj_ref, sub_ref, slope_ref, fc_ref):
    rows, cp, width_p = own_ref.shape
    first = lax.axis_index("lat") * rows
    ext = (
        [prev_ref[e] for e in range(HALF)]
        + [own_ref[e] for e in range(rows)]
        + [next_ref[e] for e in range(HALF)]
    )
    for i in range(rows):
        g = first + i
        step = step_ref[g]
        weights = jnp.concatenate(
            [
                jnp.concatenate(
                    [table_ref[0, basis_ref[g * TAPS * TAPS + a * TAPS + b]] for a in range(TAPS)],
                    axis=1,
                )
                for b in range(TAPS)
            ],
            axis=0,
        )
        stacked = jnp.concatenate(ext[i : i + TAPS], axis=0)
        taps = jnp.dot(weights, stacked, preferred_element_type=jnp.float32)
        total = taps[HALF * cp : (HALF + 1) * cp]
        for b in range(TAPS):
            if b == HALF:
                continue
            shift = lax.rem((HALF - b) * step + width_p, width_p)
            total = total + pltpu.roll(taps[b * cp : (b + 1) * cp], shift, 1)
        filtered = total * quad_ref[g]
        slope_ref[i] = gelu_grad(filtered)
        activated = gelu(filtered).astype(jnp.bfloat16)
        coarse = jnp.dot(
            proj_ref[...], activated, preferred_element_type=jnp.float32
        ).astype(jnp.bfloat16)
        forecast = jnp.dot(
            sub_ref[...], coarse, preferred_element_type=jnp.float32
        ).astype(jnp.bfloat16)
        blocks, block = fc_ref.shape[0], fc_ref.shape[3]
        for q in range(blocks):
            fc_ref[q, i] = forecast[:, q * block : (q + 1) * block]


def score_kernel(sub_ref, weight_ref, fc_ref, truth_ref, out_ref):
    members, rows, cells, block = fc_ref.shape
    vp = out_ref.shape[2]
    variables = sub_ref.shape[0] // cells
    subcells = cells // variables
    total_rows = weight_ref.shape[0] // subcells
    first = lax.axis_index("lat") * rows
    cell_sub = lax.broadcasted_iota(jnp.int32, (cells, 1), 0) // variables
    for i in range(rows):
        g = first + i
        scale = jnp.zeros((cells, 1), jnp.float32)
        for s in range(subcells):
            scale = jnp.where(cell_sub == s, weight_ref[s * total_rows + g], scale)
        truth = truth_ref[i]
        values = [fc_ref[n, i].astype(jnp.float32) for n in range(members)]
        spread = [jnp.zeros((cells, block), jnp.float32) for _ in range(members)]
        for m in range(members):
            for n in range(m + 1, members):
                term = softened_sign(values[m] - values[n])
                spread[m] = spread[m] + term
                spread[n] = spread[n] - term
        for m in range(members):
            grad = scale * (softened_sign(values[m] - truth) - spread[m] / members)
            coarse = []
            for u in range(vp):
                if u >= variables:
                    coarse.append(jnp.zeros((1, block), jnp.float32))
                    continue
                acc = None
                for r in range(cells):
                    term = sub_ref[r * variables + u] * grad[r : r + 1]
                    acc = term if acc is None else acc + term
                coarse.append(acc)
            out_ref[m, i] = jnp.concatenate(coarse, axis=0).astype(out_ref.dtype)


def ring_row(blocks_ref, i, width_p):
    row = jnp.concatenate([blocks_ref[q, i] for q in range(blocks_ref.shape[0])], axis=1)
    width = row.shape[1]
    extra = width_p - width
    lo = extra // 2
    hi = extra - lo
    return jnp.concatenate([row, row[:, :lo], row[:, width - hi :]], axis=1)


def backward_kernel(basis_ref, step_ref, quad_ref, gc_prev_ref, gc_own_ref, gc_next_ref,
                    sl_prev_ref, sl_own_ref, sl_next_ref, proj_t_ref, table_ref, out_ref):
    rows, cp, width_p = sl_own_ref.shape
    channels, width = out_ref.shape[1], out_ref.shape[2]
    total_rows = step_ref.shape[0]
    first = lax.axis_index("lat") * rows
    sources = (
        [(gc_prev_ref, sl_prev_ref, e) for e in range(HALF)]
        + [(gc_own_ref, sl_own_ref, e) for e in range(rows)]
        + [(gc_next_ref, sl_next_ref, e) for e in range(HALF)]
    )
    acc = [None] * rows
    for e in range(rows + 2 * HALF):
        a_lo = max(0, 2 * HALF - e)
        a_hi = min(TAPS - 1, rows - 1 + 2 * HALF - e)
        if a_lo > a_hi:
            continue
        g = jnp.clip(first - HALF + e, 0, total_rows - 1)
        step = step_ref[g]
        weights = jnp.concatenate(
            [
                jnp.concatenate(
                    [table_ref[1, basis_ref[g * TAPS * TAPS + a * TAPS + b]] for b in range(TAPS)],
                    axis=1,
                )
                for a in range(a_lo, a_hi + 1)
            ],
            axis=0,
        )
        gc_ref, sl_ref, r = sources[e]
        grad_act = jnp.dot(
            proj_t_ref[...], ring_row(gc_ref, r, width_p).astype(jnp.bfloat16),
            preferred_element_type=jnp.float32,
        )
        source = (grad_act * sl_ref[r]).astype(jnp.bfloat16)
        rolled = []
        for b in range(TAPS):
            if b == HALF:
                rolled.append(source)
            else:
                shift = lax.rem((b - HALF) * step + width_p, width_p)
                rolled.append(pltpu.roll(source, shift, 1))
        stacked = jnp.concatenate(rolled, axis=0)
        part = jnp.dot(weights, stacked, preferred_element_type=jnp.float32)
        scale = quad_ref[g]
        for a in range(a_lo, a_hi + 1):
            i2 = e + a - 2 * HALF
            piece = part[(a - a_lo) * cp : (a - a_lo + 1) * cp] * scale
            acc[i2] = piece if acc[i2] is None else acc[i2] + piece
    for i2 in range(rows):
        out_ref[i2] = acc[i2][:channels, :width].astype(out_ref.dtype)


def vmem():
    return pl.BlockSpec(memory_space=pltpu.VMEM)


def smem():
    return pl.BlockSpec(memory_space=pltpu.SMEM)


def on_device(latents, filters, project, subcell_maps, verifying_truth, basis_rows, step_rows):
    rows = latents.shape[1]
    channels = latents.shape[2]
    width = latents.shape[3]
    variables = project.shape[0]
    subcells = subcell_maps.shape[0]
    cp = round_up(channels, 16)
    vp = round_up(variables, 16)
    svp = subcells * variables
    width_p = ring_width(width)
    total_rows = rows * lax.axis_size("lat")
    first = lax.axis_index("lat") * rows

    quad_all = latitude_rows(total_rows, total_rows)
    weight_all = subcell_weight(0, total_rows, total_rows).reshape(-1)
    sub_flat = subcell_maps.astype(jnp.float32).reshape(-1)
    blocks = lax.axis_size("member")
    block = width // blocks
    truth = verifying_truth.reshape(subcells * variables, rows, block).transpose(1, 0, 2)

    table = jnp.concatenate([filters, jnp.zeros((1,) + filters.shape[1:], filters.dtype)], 0)
    table = pad_axis(pad_axis(table, 1, cp), 2, cp)
    tables = jnp.stack([table, table.transpose(0, 2, 1)])
    basis_flat = basis_rows.reshape(-1)

    proj_p = pad_axis(pad_axis(project, 0, vp), 1, cp)
    sub_p = pad_axis(pad_axis(subcell_maps.reshape(subcells * variables, variables), 0, svp), 1, vp)

    own = to_ring(pad_axis(latents[0], 1, cp), width_p)
    low, high = halo(own, "lat", HALF)

    slope, fc = pl.pallas_call(
        forward_kernel,
        out_shape=(
            jax.ShapeDtypeStruct((rows, cp, width_p), jnp.float32),
            jax.ShapeDtypeStruct((blocks, rows, svp, block), jnp.bfloat16),
        ),
        in_specs=[smem(), smem(), smem()] + [vmem()] * 6,
        out_specs=(vmem(), vmem()),
    )(basis_flat, step_rows, quad_all, low, own, high, tables, proj_p, sub_p)

    fc_owned = lax.all_to_all(fc, "member", split_axis=0, concat_axis=0, tiled=True)
    gc_owned = pl.pallas_call(
        score_kernel,
        out_shape=jax.ShapeDtypeStruct((blocks, rows, vp, block), jnp.bfloat16),
        in_specs=[smem(), smem()] + [vmem()] * 2,
        out_specs=vmem(),
    )(sub_flat, weight_all, fc_owned, truth)
    gc_home = lax.all_to_all(gc_owned, "member", split_axis=0, concat_axis=0, tiled=True)
    proj_t = pad_axis(pad_axis(project.T, 0, cp), 1, vp)
    sl_low, sl_high = halo(slope, "lat", HALF)
    gc_low, gc_high = halo(gc_home, "lat", HALF, axis=1)
    result = pl.pallas_call(
        backward_kernel,
        out_shape=jax.ShapeDtypeStruct((rows, channels, width), jnp.bfloat16),
        in_specs=[smem(), smem(), smem()] + [vmem()] * 8,
        out_specs=vmem(),
    )(basis_flat, step_rows, quad_all, gc_low, gc_home, gc_high, sl_low, slope, sl_high,
      proj_t, tables)
    return result[None]


def solution(mesh):
    placed = (
        P("member", "lat", None, None),
        P(),
        P(),
        P(),
        P(None, None, "lat", "member"),
        P(),
        P(),
    )
    return jax.shard_map(
        on_device,
        mesh=mesh,
        in_specs=placed,
        out_specs=P("member", "lat", None, None),
        check_vma=False,
    )
```

```python
import jax
import jax.numpy as jnp
from jax import lax
from jax.experimental import pallas as pl
from jax.experimental.pallas import tpu as pltpu
from jax.sharding import PartitionSpec as P

TAPS = 7
HALF = 3
MAX_STEP = 3


def round_up(value, unit):
    return (value + unit - 1) // unit * unit


def ring_width(width):
    return round_up(width + 4 * HALF * MAX_STEP + 2, 128)


def to_ring(block, width_p):
    width = block.shape[-1]
    extra = width_p - width
    lo = extra // 2
    hi = extra - lo
    return jnp.concatenate(
        [block, block[..., :lo], block[..., width - hi :]], axis=-1
    )


def pad_axis(block, axis, size):
    pads = [(0, 0)] * block.ndim
    pads[axis] = (0, size - block.shape[axis])
    return jnp.pad(block, pads)


def halo(block, axis_name, width, axis=0):
    count = lax.axis_size(axis_name)
    forward = [(i, i + 1) for i in range(count - 1)]
    backward = [(target, source) for source, target in forward]
    size = block.shape[axis]
    low = lax.ppermute(lax.slice_in_dim(block, size - width, size, axis=axis), axis_name, forward)
    high = lax.ppermute(lax.slice_in_dim(block, 0, width, axis=axis), axis_name, backward)
    return low, high


def latitude_rows(count, total):
    rows = jnp.arange(count, dtype=jnp.int32).astype(jnp.float32)
    return jnp.cos(((rows + 0.5) / total - 0.5) * jnp.pi)


def subcell_weight(first, count, total):
    rows = (first + jnp.arange(count, dtype=jnp.int32)).astype(jnp.float32)
    sub_row = jnp.array([0.0, 0.0, 1.0, 1.0], jnp.float32)
    fine = 2.0 * rows[None, :] + sub_row[:, None]
    return jnp.cos(((fine + 0.5) / (2.0 * total) - 0.5) * jnp.pi)


def softened_sign(diff):
    return diff / jnp.sqrt(diff * diff + 0.01)


SQRT_2_OVER_PI = 0.7978845608028654


def gelu(x):
    inner = SQRT_2_OVER_PI * (x + 0.044715 * (x * x * x))
    return x * (0.5 * (1.0 + jnp.tanh(inner)))


def gelu_grad(x):
    inner = SQRT_2_OVER_PI * (x + 0.044715 * (x * x * x))
    t = jnp.tanh(inner)
    d_inner = SQRT_2_OVER_PI * (1.0 + 3.0 * 0.044715 * (x * x))
    return 0.5 * (1.0 + t) + x * (0.5 * (1.0 - t * t)) * d_inner


def forward_kernel(basis_ref, step_ref, quad_ref, prev_ref, own_ref, next_ref, table_ref,
                   proj_ref, sub_ref, slope_ref, fc_ref):
    rows, cp, width_p = own_ref.shape
    first = lax.axis_index("lat") * rows
    ext = (
        [prev_ref[e] for e in range(HALF)]
        + [own_ref[e] for e in range(rows)]
        + [next_ref[e] for e in range(HALF)]
    )
    for i in range(rows):
        g = first + i
        step = step_ref[g]
        weights = jnp.concatenate(
            [
                jnp.concatenate(
                    [table_ref[0, basis_ref[g * TAPS * TAPS + a * TAPS + b]] for a in range(TAPS)],
                    axis=1,
                )
                for b in range(TAPS)
            ],
            axis=0,
        )
        stacked = jnp.concatenate(ext[i : i + TAPS], axis=0)
        taps = jnp.dot(weights, stacked, preferred_element_type=jnp.float32)
        total = taps[HALF * cp : (HALF + 1) * cp]
        for b in range(TAPS):
            if b == HALF:
                continue
            shift = lax.rem((HALF - b) * step + width_p, width_p)
            total = total + pltpu.roll(taps[b * cp : (b + 1) * cp], shift, 1)
        filtered = total * quad_ref[g]
        slope_ref[i] = gelu_grad(filtered)
        activated = gelu(filtered).astype(jnp.bfloat16)
        coarse = jnp.dot(
            proj_ref[...], activated, preferred_element_type=jnp.float32
        ).astype(jnp.bfloat16)
        forecast = jnp.dot(
            sub_ref[...], coarse, preferred_element_type=jnp.float32
        ).astype(jnp.bfloat16)
        blocks, block = fc_ref.shape[0], fc_ref.shape[3]
        for q in range(blocks):
            fc_ref[q, i] = forecast[:, q * block : (q + 1) * block]


def score_kernel(sub_ref, weight_ref, fc_ref, truth_ref, out_ref):
    members, rows, cells, block = fc_ref.shape
    bands, vp = out_ref.shape[1], out_ref.shape[3]
    band = lax.axis_index("lat")
    variables = sub_ref.shape[0] // cells
    subcells = cells // variables
    total_rows = weight_ref.shape[0] // subcells
    first = lax.axis_index("lat") * rows
    cell_sub = lax.broadcasted_iota(jnp.int32, (cells, 1), 0) // variables
    for i in range(rows):
        g = first + i
        scale = jnp.zeros((cells, 1), jnp.float32)
        for s in range(subcells):
            scale = jnp.where(cell_sub == s, weight_ref[s * total_rows + g], scale)
        truth = truth_ref[i]
        values = [fc_ref[n, i].astype(jnp.float32) for n in range(members)]
        spread = [jnp.zeros((cells, block), jnp.float32) for _ in range(members)]
        for m in range(members):
            for n in range(m + 1, members):
                term = softened_sign(values[m] - values[n])
                spread[m] = spread[m] + term
                spread[n] = spread[n] - term
        for m in range(members):
            grad = scale * (softened_sign(values[m] - truth) - spread[m] / members)
            coarse = []
            for u in range(vp):
                if u >= variables:
                    coarse.append(jnp.zeros((1, block), jnp.float32))
                    continue
                acc = None
                for r in range(cells):
                    term = sub_ref[r * variables + u] * grad[r : r + 1]
                    acc = term if acc is None else acc + term
                coarse.append(acc)
            coarse = jnp.concatenate(coarse, axis=0).astype(out_ref.dtype)
            for lp in range(bands):
                near = jnp.abs(lp - band) <= 1
                out_ref[m, lp, i] = jnp.where(near, coarse, jnp.zeros_like(coarse))


def ring_row(blocks_ref, band, i, width_p):
    row = jnp.concatenate(
        [blocks_ref[q, band, i] for q in range(blocks_ref.shape[0])], axis=1
    )
    width = row.shape[1]
    extra = width_p - width
    lo = extra // 2
    hi = extra - lo
    return jnp.concatenate([row, row[:, :lo], row[:, width - hi :]], axis=1)


def backward_kernel(basis_ref, step_ref, quad_ref, gc_ref, sl_prev_ref, sl_own_ref,
                    sl_next_ref, proj_t_ref, table_ref, out_ref):
    rows, cp, width_p = sl_own_ref.shape
    bands = gc_ref.shape[1]
    channels, width = out_ref.shape[1], out_ref.shape[2]
    total_rows = step_ref.shape[0]
    band = lax.axis_index("lat")
    first = band * rows
    below = jnp.maximum(band - 1, 0)
    above = jnp.minimum(band + 1, bands - 1)
    sources = (
        [(below, sl_prev_ref, rows - HALF + e, e) for e in range(HALF)]
        + [(band, sl_own_ref, e, e) for e in range(rows)]
        + [(above, sl_next_ref, e, e) for e in range(HALF)]
    )
    acc = [None] * rows
    for e in range(rows + 2 * HALF):
        a_lo = max(0, 2 * HALF - e)
        a_hi = min(TAPS - 1, rows - 1 + 2 * HALF - e)
        if a_lo > a_hi:
            continue
        g = jnp.clip(first - HALF + e, 0, total_rows - 1)
        step = step_ref[g]
        weights = jnp.concatenate(
            [
                jnp.concatenate(
                    [table_ref[1, basis_ref[g * TAPS * TAPS + a * TAPS + b]] for b in range(TAPS)],
                    axis=1,
                )
                for a in range(a_lo, a_hi + 1)
            ],
            axis=0,
        )
        src_band, sl_ref, r, rs = sources[e]
        grad_act = jnp.dot(
            proj_t_ref[...], ring_row(gc_ref, src_band, r, width_p).astype(jnp.bfloat16),
            preferred_element_type=jnp.float32,
        )
        source = (grad_act * sl_ref[rs]).astype(jnp.bfloat16)
        rolled = []
        for b in range(TAPS):
            if b == HALF:
                rolled.append(source)
            else:
                shift = lax.rem((b - HALF) * step + width_p, width_p)
                rolled.append(pltpu.roll(source, shift, 1))
        stacked = jnp.concatenate(rolled, axis=0)
        part = jnp.dot(weights, stacked, preferred_element_type=jnp.float32)
        scale = quad_ref[g]
        for a in range(a_lo, a_hi + 1):
            i2 = e + a - 2 * HALF
            piece = part[(a - a_lo) * cp : (a - a_lo + 1) * cp] * scale
            acc[i2] = piece if acc[i2] is None else acc[i2] + piece
    for i2 in range(rows):
        out_ref[i2] = acc[i2][:channels, :width].astype(out_ref.dtype)


def vmem():
    return pl.BlockSpec(memory_space=pltpu.VMEM)


def smem():
    return pl.BlockSpec(memory_space=pltpu.SMEM)


def on_device(latents, filters, project, subcell_maps, verifying_truth, basis_rows, step_rows):
    rows = latents.shape[1]
    channels = latents.shape[2]
    width = latents.shape[3]
    variables = project.shape[0]
    subcells = subcell_maps.shape[0]
    cp = round_up(channels, 16)
    vp = round_up(variables, 16)
    svp = subcells * variables
    width_p = ring_width(width)
    total_rows = rows * lax.axis_size("lat")
    first = lax.axis_index("lat") * rows

    quad_all = latitude_rows(total_rows, total_rows)
    weight_all = subcell_weight(0, total_rows, total_rows).reshape(-1)
    sub_flat = subcell_maps.astype(jnp.float32).reshape(-1)
    blocks = lax.axis_size("member")
    bands = lax.axis_size("lat")
    block = width // blocks
    truth = verifying_truth.reshape(subcells * variables, rows, block).transpose(1, 0, 2)

    table = jnp.concatenate([filters, jnp.zeros((1,) + filters.shape[1:], filters.dtype)], 0)
    table = pad_axis(pad_axis(table, 1, cp), 2, cp)
    tables = jnp.stack([table, table.transpose(0, 2, 1)])
    basis_flat = basis_rows.reshape(-1)

    proj_p = pad_axis(pad_axis(project, 0, vp), 1, cp)
    sub_p = pad_axis(pad_axis(subcell_maps.reshape(subcells * variables, variables), 0, svp), 1, vp)

    own = to_ring(pad_axis(latents[0], 1, cp), width_p)
    low, high = halo(own, "lat", HALF)

    slope, fc = pl.pallas_call(
        forward_kernel,
        out_shape=(
            jax.ShapeDtypeStruct((rows, cp, width_p), jnp.float32),
            jax.ShapeDtypeStruct((blocks, rows, svp, block), jnp.bfloat16),
        ),
        in_specs=[smem(), smem(), smem()] + [vmem()] * 6,
        out_specs=(vmem(), vmem()),
    )(basis_flat, step_rows, quad_all, low, own, high, tables, proj_p, sub_p)

    fc_owned = lax.all_to_all(fc, "member", split_axis=0, concat_axis=0, tiled=True)
    gc_owned = pl.pallas_call(
        score_kernel,
        out_shape=jax.ShapeDtypeStruct((blocks, bands, rows, vp, block), jnp.bfloat16),
        in_specs=[smem(), smem()] + [vmem()] * 2,
        out_specs=vmem(),
    )(sub_flat, weight_all, fc_owned, truth)
    gc_home = lax.all_to_all(
        gc_owned.reshape((blocks * bands,) + gc_owned.shape[2:]),
        ("member", "lat"), split_axis=0, concat_axis=0, tiled=True,
    ).reshape(gc_owned.shape)
    proj_t = pad_axis(pad_axis(project.T, 0, cp), 1, vp)
    sl_low, sl_high = halo(slope, "lat", HALF)
    result = pl.pallas_call(
        backward_kernel,
        out_shape=jax.ShapeDtypeStruct((rows, channels, width), jnp.bfloat16),
        in_specs=[smem(), smem(), smem()] + [vmem()] * 6,
        out_specs=vmem(),
    )(basis_flat, step_rows, quad_all, gc_home, sl_low, slope, sl_high, proj_t, tables)
    return result[None]


def solution(mesh):
    placed = (
        P("member", "lat", None, None),
        P(),
        P(),
        P(),
        P(None, None, "lat", "member"),
        P(),
        P(),
    )
    return jax.shard_map(
        on_device,
        mesh=mesh,
        in_specs=placed,
        out_specs=P("member", "lat", None, None),
        check_vma=False,
    )
```

```python
import functools

import jax
import jax.numpy as jnp
from jax import lax
from jax.experimental import pallas as pl
from jax.experimental.pallas import tpu as pltpu
from jax.sharding import PartitionSpec as P

TAPS = 7
HALF = 3
MAX_STEP = 3


def round_up(value, unit):
    return (value + unit - 1) // unit * unit


def ring_width(width):
    return round_up(width + 4 * HALF * MAX_STEP + 2, 128)


def to_ring(block, width_p):
    width = block.shape[-1]
    extra = width_p - width
    lo = extra // 2
    hi = extra - lo
    return jnp.concatenate(
        [block, block[..., :lo], block[..., width - hi :]], axis=-1
    )


def pad_axis(block, axis, size):
    pads = [(0, 0)] * block.ndim
    pads[axis] = (0, size - block.shape[axis])
    return jnp.pad(block, pads)


def halo(block, axis_name, width):
    count = lax.axis_size(axis_name)
    forward = [(i, i + 1) for i in range(count - 1)]
    backward = [(target, source) for source, target in forward]
    low = lax.ppermute(block[block.shape[0] - width :], axis_name, forward)
    high = lax.ppermute(block[:width], axis_name, backward)
    return low, high


def latitude_rows(count, total):
    rows = jnp.arange(count, dtype=jnp.int32).astype(jnp.float32)
    return jnp.cos(((rows + 0.5) / total - 0.5) * jnp.pi)


def subcell_weight(first, count, total):
    rows = (first + jnp.arange(count, dtype=jnp.int32)).astype(jnp.float32)
    sub_row = jnp.array([0.0, 0.0, 1.0, 1.0], jnp.float32)
    fine = 2.0 * rows[None, :] + sub_row[:, None]
    return jnp.cos(((fine + 0.5) / (2.0 * total) - 0.5) * jnp.pi)


def softened_sign(diff):
    return diff / jnp.sqrt(diff * diff + 0.01)


SQRT_2_OVER_PI = 0.7978845608028654


def gelu(x):
    inner = SQRT_2_OVER_PI * (x + 0.044715 * (x * x * x))
    return x * (0.5 * (1.0 + jnp.tanh(inner)))


def gelu_grad(x):
    inner = SQRT_2_OVER_PI * (x + 0.044715 * (x * x * x))
    t = jnp.tanh(inner)
    d_inner = SQRT_2_OVER_PI * (1.0 + 3.0 * 0.044715 * (x * x))
    return 0.5 * (1.0 + t) + x * (0.5 * (1.0 - t * t)) * d_inner


def gelu_and_grad(x):
    inner = SQRT_2_OVER_PI * (x + 0.044715 * (x * x * x))
    t = jnp.tanh(inner)
    d_inner = SQRT_2_OVER_PI * (1.0 + 3.0 * 0.044715 * (x * x))
    half = 0.5 * (1.0 + t)
    return x * half, half + x * (0.5 * (1.0 - t * t)) * d_inner


def forward_kernel(basis_ref, step_ref, quad_ref, prev_ref, own_ref, next_ref, table_ref,
                   proj_ref, sub_ref, slope_ref, fc_ref):
    rows, cp, width_p = own_ref.shape
    first = lax.axis_index("lat") * rows
    ext = (
        [prev_ref[e] for e in range(HALF)]
        + [own_ref[e] for e in range(rows)]
        + [next_ref[e] for e in range(HALF)]
    )
    for i in range(rows):
        g = first + i
        step = step_ref[g]
        weights = jnp.concatenate(
            [
                jnp.concatenate(
                    [table_ref[0, basis_ref[g * TAPS * TAPS + a * TAPS + b]] for a in range(TAPS)],
                    axis=1,
                )
                for b in range(TAPS)
            ],
            axis=0,
        )
        stacked = jnp.concatenate(ext[i : i + TAPS], axis=0)
        taps = jnp.dot(weights, stacked, preferred_element_type=jnp.float32)
        total = taps[HALF * cp : (HALF + 1) * cp]
        for b in range(TAPS):
            if b == HALF:
                continue
            shift = lax.rem((HALF - b) * step + width_p, width_p)
            total = total + pltpu.roll(taps[b * cp : (b + 1) * cp], shift, 1)
        filtered = total * quad_ref[g]
        gelu_value, gelu_slope = gelu_and_grad(filtered)
        slope_ref[i] = gelu_slope
        activated = gelu_value.astype(jnp.bfloat16)
        coarse = jnp.dot(
            proj_ref[...], activated, preferred_element_type=jnp.float32
        ).astype(jnp.bfloat16)
        forecast = jnp.dot(
            sub_ref[...], coarse, preferred_element_type=jnp.float32
        ).astype(jnp.bfloat16)
        blocks, block = fc_ref.shape[0], fc_ref.shape[3]
        for q in range(blocks):
            fc_ref[q, i] = forecast[:, q * block : (q + 1) * block]


def split3(x):
    hi = x.astype(jnp.bfloat16)
    rest = x - hi.astype(jnp.float32)
    mid = rest.astype(jnp.bfloat16)
    lo = (rest - mid.astype(jnp.float32)).astype(jnp.bfloat16)
    return hi, mid, lo


def score_kernel(subcells, weight_ref, sub_t_ref, fc_ref, truth_ref, out_ref):
    members, rows, cells, block = fc_ref.shape
    total_rows = weight_ref.shape[0] // subcells
    slot = 128
    lanes = members * slot
    first = lax.axis_index("lat") * rows
    variables = cells // subcells
    cell_sub = lax.broadcasted_iota(jnp.int32, (cells, 1), 0) // variables
    pad = jnp.zeros((cells, slot - block), jnp.float32)
    for i in range(rows):
        g = first + i
        scale = jnp.zeros((cells, 1), jnp.float32)
        for s in range(subcells):
            scale = jnp.where(cell_sub == s, weight_ref[s * total_rows + g], scale)
        values = jnp.concatenate(
            [
                jnp.concatenate([fc_ref[n, i].astype(jnp.float32), pad], axis=1)
                for n in range(members)
            ],
            axis=1,
        )
        truth_slot = jnp.concatenate([truth_ref[i], pad], axis=1)
        truth = jnp.concatenate([truth_slot] * members, axis=1)
        spread = jnp.zeros((cells, lanes), jnp.float32)
        for k in range(1, (members + 1) // 2):
            term = softened_sign(values - pltpu.roll(values, k * slot, 1))
            spread = spread + term - pltpu.roll(term, lanes - k * slot, 1)
        if members % 2 == 0:
            spread = spread + softened_sign(
                values - pltpu.roll(values, (members // 2) * slot, 1)
            )
        grad = scale * (softened_sign(values - truth) - spread / members)
        coarse = None
        for part in split3(grad):
            term = jnp.dot(sub_t_ref[...], part, preferred_element_type=jnp.float32)
            coarse = term if coarse is None else coarse + term
        coarse = coarse.astype(out_ref.dtype)
        for m in range(members):
            out_ref[m, i] = coarse[:, m * slot : m * slot + block]


def grad_filtered_kernel(gc_ref, slope_ref, proj_t_ref, out_ref):
    blocks, rows = gc_ref.shape[0], gc_ref.shape[1]
    width_p = slope_ref.shape[2]
    for i in range(rows):
        row = jnp.concatenate([gc_ref[q, i] for q in range(blocks)], axis=1)
        width = row.shape[1]
        extra = width_p - width
        lo = extra // 2
        hi = extra - lo
        ring = jnp.concatenate([row, row[:, :lo], row[:, width - hi :]], axis=1)
        grad_act = jnp.dot(proj_t_ref[...], ring, preferred_element_type=jnp.float32)
        out_ref[i] = (grad_act * slope_ref[i]).astype(jnp.bfloat16)


def backward_kernel(basis_ref, step_ref, quad_ref, prev_ref, own_ref, next_ref, table_ref,
                    out_ref):
    rows, cp, width_p = own_ref.shape
    channels, width = out_ref.shape[1], out_ref.shape[2]
    total_rows = step_ref.shape[0]
    first = lax.axis_index("lat") * rows
    ext = (
        [prev_ref[e] for e in range(HALF)]
        + [own_ref[e] for e in range(rows)]
        + [next_ref[e] for e in range(HALF)]
    )
    acc = [None] * rows
    for e in range(rows + 2 * HALF):
        a_lo = max(0, 2 * HALF - e)
        a_hi = min(TAPS - 1, rows - 1 + 2 * HALF - e)
        if a_lo > a_hi:
            continue
        g = jnp.clip(first - HALF + e, 0, total_rows - 1)
        step = step_ref[g]
        weights = jnp.concatenate(
            [
                jnp.concatenate(
                    [table_ref[1, basis_ref[g * TAPS * TAPS + a * TAPS + b]] for b in range(TAPS)],
                    axis=1,
                )
                for a in range(a_lo, a_hi + 1)
            ],
            axis=0,
        )
        source = ext[e]
        rolled = []
        for b in range(TAPS):
            if b == HALF:
                rolled.append(source)
            else:
                shift = lax.rem((b - HALF) * step + width_p, width_p)
                rolled.append(pltpu.roll(source, shift, 1))
        stacked = jnp.concatenate(rolled, axis=0)
        part = jnp.dot(weights, stacked, preferred_element_type=jnp.float32)
        scale = quad_ref[g]
        for a in range(a_lo, a_hi + 1):
            i2 = e + a - 2 * HALF
            piece = part[(a - a_lo) * cp : (a - a_lo + 1) * cp] * scale
            acc[i2] = piece if acc[i2] is None else acc[i2] + piece
    for i2 in range(rows):
        out_ref[i2] = acc[i2][:channels, :width].astype(out_ref.dtype)


def vmem():
    return pl.BlockSpec(memory_space=pltpu.VMEM)


def smem():
    return pl.BlockSpec(memory_space=pltpu.SMEM)


def on_device(latents, filters, project, subcell_maps, verifying_truth, basis_rows, step_rows):
    rows = latents.shape[1]
    channels = latents.shape[2]
    width = latents.shape[3]
    variables = project.shape[0]
    subcells = subcell_maps.shape[0]
    cp = round_up(channels, 16)
    vp = round_up(variables, 16)
    svp = subcells * variables
    width_p = ring_width(width)
    total_rows = rows * lax.axis_size("lat")
    first = lax.axis_index("lat") * rows

    quad_all = latitude_rows(total_rows, total_rows)
    weight_all = subcell_weight(0, total_rows, total_rows).reshape(-1)
    sub_t = pad_axis(subcell_maps.reshape(subcells * variables, variables).T, 0, vp)
    blocks = lax.axis_size("member")
    block = width // blocks
    truth = verifying_truth.reshape(subcells * variables, rows, block).transpose(1, 0, 2)

    table = jnp.concatenate([filters, jnp.zeros((1,) + filters.shape[1:], filters.dtype)], 0)
    table = pad_axis(pad_axis(table, 1, cp), 2, cp)
    tables = jnp.stack([table, table.transpose(0, 2, 1)])
    basis_flat = basis_rows.reshape(-1)

    proj_p = pad_axis(pad_axis(project, 0, vp), 1, cp)
    sub_p = pad_axis(pad_axis(subcell_maps.reshape(subcells * variables, variables), 0, svp), 1, vp)

    own = to_ring(pad_axis(latents[0], 1, cp), width_p)
    low, high = halo(own, "lat", HALF)

    slope, fc = pl.pallas_call(
        forward_kernel,
        out_shape=(
            jax.ShapeDtypeStruct((rows, cp, width_p), jnp.float32),
            jax.ShapeDtypeStruct((blocks, rows, svp, block), jnp.bfloat16),
        ),
        in_specs=[smem(), smem(), smem()] + [vmem()] * 6,
        out_specs=(vmem(), vmem()),
    )(basis_flat, step_rows, quad_all, low, own, high, tables, proj_p, sub_p)

    fc_owned = lax.all_to_all(fc, "member", split_axis=0, concat_axis=0, tiled=True)
    gc_owned = pl.pallas_call(
        functools.partial(score_kernel, subcells),
        out_shape=jax.ShapeDtypeStruct((blocks, rows, vp, block), jnp.bfloat16),
        in_specs=[smem()] + [vmem()] * 3,
        out_specs=vmem(),
    )(weight_all, sub_t, fc_owned, truth)
    gc_home = lax.all_to_all(gc_owned, "member", split_axis=0, concat_axis=0, tiled=True)
    proj_t = pad_axis(pad_axis(project.T, 0, cp), 1, vp)
    grad_filtered = pl.pallas_call(
        grad_filtered_kernel,
        out_shape=jax.ShapeDtypeStruct((rows, cp, width_p), jnp.bfloat16),
        in_specs=[vmem()] * 3,
        out_specs=vmem(),
    )(gc_home, slope, proj_t)

    g_low, g_high = halo(grad_filtered, "lat", HALF)
    result = pl.pallas_call(
        backward_kernel,
        out_shape=jax.ShapeDtypeStruct((rows, channels, width), jnp.bfloat16),
        in_specs=[smem(), smem(), smem()] + [vmem()] * 4,
        out_specs=vmem(),
    )(basis_flat, step_rows, quad_all, g_low, grad_filtered, g_high, tables)
    return result[None]


def solution(mesh):
    placed = (
        P("member", "lat", None, None),
        P(),
        P(),
        P(),
        P(None, None, "lat", "member"),
        P(),
        P(),
    )
    return jax.shard_map(
        on_device,
        mesh=mesh,
        in_specs=placed,
        out_specs=P("member", "lat", None, None),
        check_vma=False,
    )
```

```python
import functools

import jax
import jax.numpy as jnp
from jax import lax
from jax.experimental import pallas as pl
from jax.experimental.pallas import tpu as pltpu
from jax.sharding import PartitionSpec as P

TAPS = 7
HALF = 3
MAX_STEP = 3


def round_up(value, unit):
    return (value + unit - 1) // unit * unit


def ring_width(width):
    return round_up(width + 4 * HALF * MAX_STEP + 2, 128)


def to_ring(block, width_p):
    width = block.shape[-1]
    extra = width_p - width
    lo = extra // 2
    hi = extra - lo
    return jnp.concatenate(
        [block, block[..., :lo], block[..., width - hi :]], axis=-1
    )


def pad_axis(block, axis, size):
    pads = [(0, 0)] * block.ndim
    pads[axis] = (0, size - block.shape[axis])
    return jnp.pad(block, pads)


def halo(block, axis_name, width):
    count = lax.axis_size(axis_name)
    forward = [(i, i + 1) for i in range(count - 1)]
    backward = [(target, source) for source, target in forward]
    low = lax.ppermute(block[block.shape[0] - width :], axis_name, forward)
    high = lax.ppermute(block[:width], axis_name, backward)
    return low, high


def latitude_rows(count, total):
    rows = jnp.arange(count, dtype=jnp.int32).astype(jnp.float32)
    return jnp.cos(((rows + 0.5) / total - 0.5) * jnp.pi)


def subcell_weight(first, count, total):
    rows = (first + jnp.arange(count, dtype=jnp.int32)).astype(jnp.float32)
    sub_row = jnp.array([0.0, 0.0, 1.0, 1.0], jnp.float32)
    fine = 2.0 * rows[None, :] + sub_row[:, None]
    return jnp.cos(((fine + 0.5) / (2.0 * total) - 0.5) * jnp.pi)


def softened_sign(diff):
    return diff / jnp.sqrt(diff * diff + 0.01)


SQRT_2_OVER_PI = 0.7978845608028654


def gelu(x):
    inner = SQRT_2_OVER_PI * (x + 0.044715 * (x * x * x))
    return x * (0.5 * (1.0 + jnp.tanh(inner)))


def gelu_grad(x):
    inner = SQRT_2_OVER_PI * (x + 0.044715 * (x * x * x))
    t = jnp.tanh(inner)
    d_inner = SQRT_2_OVER_PI * (1.0 + 3.0 * 0.044715 * (x * x))
    return 0.5 * (1.0 + t) + x * (0.5 * (1.0 - t * t)) * d_inner


def gelu_and_grad(x):
    inner = SQRT_2_OVER_PI * (x + 0.044715 * (x * x * x))
    t = jnp.tanh(inner)
    d_inner = SQRT_2_OVER_PI * (1.0 + 3.0 * 0.044715 * (x * x))
    half = 0.5 * (1.0 + t)
    return x * half, half + x * (0.5 * (1.0 - t * t)) * d_inner


def forward_kernel(basis_ref, step_ref, quad_ref, prev_ref, own_ref, next_ref, table_ref,
                   proj_ref, sub_ref, slope_ref, fc_ref):
    rows, cp, width_p = own_ref.shape
    first = lax.axis_index("lat") * rows
    ext = (
        [prev_ref[e] for e in range(HALF)]
        + [own_ref[e] for e in range(rows)]
        + [next_ref[e] for e in range(HALF)]
    )
    for i in range(rows):
        g = first + i
        step = step_ref[g]
        weights = jnp.concatenate(
            [
                jnp.concatenate(
                    [table_ref[0, basis_ref[g * TAPS * TAPS + a * TAPS + b]] for a in range(TAPS)],
                    axis=1,
                )
                for b in range(TAPS)
            ],
            axis=0,
        )
        stacked = jnp.concatenate(ext[i : i + TAPS], axis=0)
        taps = jnp.dot(weights, stacked, preferred_element_type=jnp.float32)
        total = taps[HALF * cp : (HALF + 1) * cp]
        for b in range(TAPS):
            if b == HALF:
                continue
            shift = lax.rem((HALF - b) * step + width_p, width_p)
            total = total + pltpu.roll(taps[b * cp : (b + 1) * cp], shift, 1)
        filtered = total * quad_ref[g]
        gelu_value, gelu_slope = gelu_and_grad(filtered)
        slope_ref[i] = gelu_slope
        activated = gelu_value.astype(jnp.bfloat16)
        coarse = jnp.dot(
            proj_ref[...], activated, preferred_element_type=jnp.float32
        ).astype(jnp.bfloat16)
        forecast = jnp.dot(
            sub_ref[...], coarse, preferred_element_type=jnp.float32
        ).astype(jnp.bfloat16)
        blocks, block = fc_ref.shape[0], fc_ref.shape[3]
        for q in range(blocks):
            fc_ref[q, i] = forecast[:, q * block : (q + 1) * block]


def split3(x):
    hi = x.astype(jnp.bfloat16)
    rest = x - hi.astype(jnp.float32)
    mid = rest.astype(jnp.bfloat16)
    lo = (rest - mid.astype(jnp.float32)).astype(jnp.bfloat16)
    return hi, mid, lo


def score_kernel(subcells, weight_ref, sub_t_ref, fc_ref, truth_ref, out_ref):
    members, rows, cells, block = fc_ref.shape
    total_rows = weight_ref.shape[0] // subcells
    slot = 128
    lanes = members * slot
    first = lax.axis_index("lat") * rows
    variables = cells // subcells
    cell_sub = lax.broadcasted_iota(jnp.int32, (cells, 1), 0) // variables
    pad = jnp.zeros((cells, slot - block), jnp.float32)
    for i in range(rows):
        g = first + i
        scale = jnp.zeros((cells, 1), jnp.float32)
        for s in range(subcells):
            scale = jnp.where(cell_sub == s, weight_ref[s * total_rows + g], scale)
        values = jnp.concatenate(
            [
                jnp.concatenate([fc_ref[n, i].astype(jnp.float32), pad], axis=1)
                for n in range(members)
            ],
            axis=1,
        )
        truth_slot = jnp.concatenate([truth_ref[i], pad], axis=1)
        truth = jnp.concatenate([truth_slot] * members, axis=1)
        spread = jnp.zeros((cells, lanes), jnp.float32)
        for k in range(1, (members + 1) // 2):
            term = softened_sign(values - pltpu.roll(values, k * slot, 1))
            spread = spread + term - pltpu.roll(term, lanes - k * slot, 1)
        if members % 2 == 0:
            spread = spread + softened_sign(
                values - pltpu.roll(values, (members // 2) * slot, 1)
            )
        grad = scale * (softened_sign(values - truth) - spread / members)
        coarse = None
        for part in split3(grad):
            term = jnp.dot(sub_t_ref[...], part, preferred_element_type=jnp.float32)
            coarse = term if coarse is None else coarse + term
        coarse = coarse.astype(out_ref.dtype)
        for m in range(members):
            out_ref[m, i] = coarse[:, m * slot : m * slot + block]


def grad_filtered_kernel(gc_ref, slope_ref, proj_t_ref, out_ref):
    blocks, rows = gc_ref.shape[0], gc_ref.shape[1]
    width_p = slope_ref.shape[2]
    for i in range(rows):
        row = jnp.concatenate([gc_ref[q, i] for q in range(blocks)], axis=1)
        width = row.shape[1]
        extra = width_p - width
        lo = extra // 2
        hi = extra - lo
        ring = jnp.concatenate([row, row[:, :lo], row[:, width - hi :]], axis=1)
        grad_act = jnp.dot(proj_t_ref[...], ring, preferred_element_type=jnp.float32)
        out_ref[i] = (grad_act * slope_ref[i]).astype(jnp.bfloat16)


def backward_terms(basis_ref, step_ref, quad_ref, table_ref, rows, sources, acc):
    total_rows = step_ref.shape[0]
    first = lax.axis_index("lat") * rows
    for e, src_ref, r in sources:
        cp, width_p = src_ref.shape[1], src_ref.shape[2]
        a_lo = max(0, 2 * HALF - e)
        a_hi = min(TAPS - 1, rows - 1 + 2 * HALF - e)
        if a_lo > a_hi:
            continue
        g = jnp.clip(first - HALF + e, 0, total_rows - 1)
        step = step_ref[g]
        weights = jnp.concatenate(
            [
                jnp.concatenate(
                    [table_ref[1, basis_ref[g * TAPS * TAPS + a * TAPS + b]] for b in range(TAPS)],
                    axis=1,
                )
                for a in range(a_lo, a_hi + 1)
            ],
            axis=0,
        )
        source = src_ref[r]
        rolled = []
        for b in range(TAPS):
            if b == HALF:
                rolled.append(source)
            else:
                shift = lax.rem((b - HALF) * step + width_p, width_p)
                rolled.append(pltpu.roll(source, shift, 1))
        stacked = jnp.concatenate(rolled, axis=0)
        part = jnp.dot(weights, stacked, preferred_element_type=jnp.float32)
        scale = quad_ref[g]
        for a in range(a_lo, a_hi + 1):
            i2 = e + a - 2 * HALF
            piece = part[(a - a_lo) * cp : (a - a_lo + 1) * cp] * scale
            acc[i2] = piece if acc[i2] is None else acc[i2] + piece
    return acc


def backward_own_kernel(basis_ref, step_ref, quad_ref, own_ref, table_ref, acc_ref):
    rows = own_ref.shape[0]
    acc = backward_terms(
        basis_ref, step_ref, quad_ref, table_ref, rows,
        [(HALF + r, own_ref, r) for r in range(rows)], [None] * rows,
    )
    for i2 in range(rows):
        acc_ref[i2] = acc[i2]


def backward_halo_kernel(basis_ref, step_ref, quad_ref, prev_ref, next_ref, acc_in_ref,
                         table_ref, out_ref):
    rows = acc_in_ref.shape[0]
    channels, width = out_ref.shape[1], out_ref.shape[2]
    acc = backward_terms(
        basis_ref, step_ref, quad_ref, table_ref, rows,
        [(e, prev_ref, e) for e in range(HALF)]
        + [(HALF + rows + e, next_ref, e) for e in range(HALF)],
        [acc_in_ref[i2] for i2 in range(rows)],
    )
    for i2 in range(rows):
        out_ref[i2] = acc[i2][:channels, :width].astype(out_ref.dtype)


def vmem():
    return pl.BlockSpec(memory_space=pltpu.VMEM)


def smem():
    return pl.BlockSpec(memory_space=pltpu.SMEM)


def on_device(latents, filters, project, subcell_maps, verifying_truth, basis_rows, step_rows):
    rows = latents.shape[1]
    channels = latents.shape[2]
    width = latents.shape[3]
    variables = project.shape[0]
    subcells = subcell_maps.shape[0]
    cp = round_up(channels, 16)
    vp = round_up(variables, 16)
    svp = subcells * variables
    width_p = ring_width(width)
    total_rows = rows * lax.axis_size("lat")
    first = lax.axis_index("lat") * rows

    quad_all = latitude_rows(total_rows, total_rows)
    weight_all = subcell_weight(0, total_rows, total_rows).reshape(-1)
    sub_t = pad_axis(subcell_maps.reshape(subcells * variables, variables).T, 0, vp)
    blocks = lax.axis_size("member")
    block = width // blocks
    truth = verifying_truth.reshape(subcells * variables, rows, block).transpose(1, 0, 2)

    table = jnp.concatenate([filters, jnp.zeros((1,) + filters.shape[1:], filters.dtype)], 0)
    table = pad_axis(pad_axis(table, 1, cp), 2, cp)
    tables = jnp.stack([table, table.transpose(0, 2, 1)])
    basis_flat = basis_rows.reshape(-1)

    proj_p = pad_axis(pad_axis(project, 0, vp), 1, cp)
    sub_p = pad_axis(pad_axis(subcell_maps.reshape(subcells * variables, variables), 0, svp), 1, vp)

    own = to_ring(pad_axis(latents[0], 1, cp), width_p)
    low, high = halo(own, "lat", HALF)

    slope, fc = pl.pallas_call(
        forward_kernel,
        out_shape=(
            jax.ShapeDtypeStruct((rows, cp, width_p), jnp.float32),
            jax.ShapeDtypeStruct((blocks, rows, svp, block), jnp.bfloat16),
        ),
        in_specs=[smem(), smem(), smem()] + [vmem()] * 6,
        out_specs=(vmem(), vmem()),
    )(basis_flat, step_rows, quad_all, low, own, high, tables, proj_p, sub_p)

    fc_owned = lax.all_to_all(fc, "member", split_axis=0, concat_axis=0, tiled=True)
    gc_owned = pl.pallas_call(
        functools.partial(score_kernel, subcells),
        out_shape=jax.ShapeDtypeStruct((blocks, rows, vp, block), jnp.bfloat16),
        in_specs=[smem()] + [vmem()] * 3,
        out_specs=vmem(),
    )(weight_all, sub_t, fc_owned, truth)
    gc_home = lax.all_to_all(gc_owned, "member", split_axis=0, concat_axis=0, tiled=True)
    proj_t = pad_axis(pad_axis(project.T, 0, cp), 1, vp)
    grad_filtered = pl.pallas_call(
        grad_filtered_kernel,
        out_shape=jax.ShapeDtypeStruct((rows, cp, width_p), jnp.bfloat16),
        in_specs=[vmem()] * 3,
        out_specs=vmem(),
    )(gc_home, slope, proj_t)

    g_low, g_high = halo(grad_filtered, "lat", HALF)
    own_terms = pl.pallas_call(
        backward_own_kernel,
        out_shape=jax.ShapeDtypeStruct((rows, cp, width_p), jnp.float32),
        in_specs=[smem(), smem(), smem()] + [vmem()] * 2,
        out_specs=vmem(),
        cost_estimate=pl.CostEstimate(
            flops=2 * rows * rows * cp * TAPS * cp * width_p,
            transcendentals=0,
            bytes_accessed=rows * cp * width_p * 6,
        ),
    )(basis_flat, step_rows, quad_all, grad_filtered, tables)
    result = pl.pallas_call(
        backward_halo_kernel,
        out_shape=jax.ShapeDtypeStruct((rows, channels, width), jnp.bfloat16),
        in_specs=[smem(), smem(), smem()] + [vmem()] * 4,
        out_specs=vmem(),
    )(basis_flat, step_rows, quad_all, g_low, g_high, own_terms, tables)
    return result[None]


def solution(mesh):
    placed = (
        P("member", "lat", None, None),
        P(),
        P(),
        P(),
        P(None, None, "lat", "member"),
        P(),
        P(),
    )
    return jax.shard_map(
        on_device,
        mesh=mesh,
        in_specs=placed,
        out_specs=P("member", "lat", None, None),
        check_vma=False,
    )
```

```python
import functools

import jax
import jax.numpy as jnp
from jax import lax
from jax.experimental import pallas as pl
from jax.experimental.pallas import tpu as pltpu
from jax.sharding import PartitionSpec as P

TAPS = 7
HALF = 3
MAX_STEP = 3


def round_up(value, unit):
    return (value + unit - 1) // unit * unit


def ring_width(width):
    return round_up(width + 4 * HALF * MAX_STEP + 2, 128)


def to_ring(block, width_p):
    width = block.shape[-1]
    extra = width_p - width
    lo = extra // 2
    hi = extra - lo
    return jnp.concatenate(
        [block, block[..., :lo], block[..., width - hi :]], axis=-1
    )


def pad_axis(block, axis, size):
    pads = [(0, 0)] * block.ndim
    pads[axis] = (0, size - block.shape[axis])
    return jnp.pad(block, pads)


def halo(block, axis_name, width):
    count = lax.axis_size(axis_name)
    forward = [(i, i + 1) for i in range(count - 1)]
    backward = [(target, source) for source, target in forward]
    low = lax.ppermute(block[block.shape[0] - width :], axis_name, forward)
    high = lax.ppermute(block[:width], axis_name, backward)
    return low, high


def latitude_rows(count, total):
    rows = jnp.arange(count, dtype=jnp.int32).astype(jnp.float32)
    return jnp.cos(((rows + 0.5) / total - 0.5) * jnp.pi)


def subcell_weight(first, count, total):
    rows = (first + jnp.arange(count, dtype=jnp.int32)).astype(jnp.float32)
    sub_row = jnp.array([0.0, 0.0, 1.0, 1.0], jnp.float32)
    fine = 2.0 * rows[None, :] + sub_row[:, None]
    return jnp.cos(((fine + 0.5) / (2.0 * total) - 0.5) * jnp.pi)


def softened_sign(diff):
    return diff / jnp.sqrt(diff * diff + 0.01)


SQRT_2_OVER_PI = 0.7978845608028654


def gelu(x):
    inner = SQRT_2_OVER_PI * (x + 0.044715 * (x * x * x))
    return x * (0.5 * (1.0 + jnp.tanh(inner)))


def gelu_grad(x):
    inner = SQRT_2_OVER_PI * (x + 0.044715 * (x * x * x))
    t = jnp.tanh(inner)
    d_inner = SQRT_2_OVER_PI * (1.0 + 3.0 * 0.044715 * (x * x))
    return 0.5 * (1.0 + t) + x * (0.5 * (1.0 - t * t)) * d_inner


def gelu_and_grad(x):
    inner = SQRT_2_OVER_PI * (x + 0.044715 * (x * x * x))
    t = jnp.tanh(inner)
    d_inner = SQRT_2_OVER_PI * (1.0 + 3.0 * 0.044715 * (x * x))
    half = 0.5 * (1.0 + t)
    return x * half, half + x * (0.5 * (1.0 - t * t)) * d_inner


def forward_taps(basis_ref, step_ref, table_ref, g, taps_a, sources):
    cp, width_p = sources[0].shape
    step = step_ref[g]
    weights = jnp.concatenate(
        [
            jnp.concatenate(
                [table_ref[0, basis_ref[g * TAPS * TAPS + a * TAPS + b]] for a in taps_a],
                axis=1,
            )
            for b in range(TAPS)
        ],
        axis=0,
    )
    stacked = jnp.concatenate(sources, axis=0)
    taps = jnp.dot(weights, stacked, preferred_element_type=jnp.float32)
    total = taps[HALF * cp : (HALF + 1) * cp]
    for b in range(TAPS):
        if b == HALF:
            continue
        shift = lax.rem((HALF - b) * step + width_p, width_p)
        total = total + pltpu.roll(taps[b * cp : (b + 1) * cp], shift, 1)
    return total


def own_taps(i, rows):
    return [a for a in range(TAPS) if HALF <= i + a < HALF + rows]


def forward_own_kernel(basis_ref, step_ref, own_ref, table_ref, part_ref):
    rows = own_ref.shape[0]
    first = lax.axis_index("lat") * rows
    for i in range(rows):
        taps_a = own_taps(i, rows)
        part_ref[i] = forward_taps(
            basis_ref, step_ref, table_ref, first + i, taps_a,
            [own_ref[i + a - HALF] for a in taps_a],
        )


def forward_kernel(basis_ref, step_ref, quad_ref, prev_ref, next_ref, part_ref, table_ref,
                   proj_ref, sub_ref, slope_ref, fc_ref):
    rows = part_ref.shape[0]
    first = lax.axis_index("lat") * rows
    for i in range(rows):
        g = first + i
        own = own_taps(i, rows)
        taps_a = [a for a in range(TAPS) if a not in own]
        sources = [
            prev_ref[i + a] if i + a < HALF else next_ref[i + a - HALF - rows]
            for a in taps_a
        ]
        total = part_ref[i] + forward_taps(basis_ref, step_ref, table_ref, g, taps_a, sources)
        filtered = total * quad_ref[g]
        gelu_value, gelu_slope = gelu_and_grad(filtered)
        slope_ref[i] = gelu_slope
        activated = gelu_value.astype(jnp.bfloat16)
        coarse = jnp.dot(
            proj_ref[...], activated, preferred_element_type=jnp.float32
        ).astype(jnp.bfloat16)
        forecast = jnp.dot(
            sub_ref[...], coarse, preferred_element_type=jnp.float32
        ).astype(jnp.bfloat16)
        blocks, block = fc_ref.shape[0], fc_ref.shape[3]
        for q in range(blocks):
            fc_ref[q, i] = forecast[:, q * block : (q + 1) * block]


def split3(x):
    hi = x.astype(jnp.bfloat16)
    rest = x - hi.astype(jnp.float32)
    mid = rest.astype(jnp.bfloat16)
    lo = (rest - mid.astype(jnp.float32)).astype(jnp.bfloat16)
    return hi, mid, lo


def score_kernel(subcells, weight_ref, sub_t_ref, fc_ref, truth_ref, out_ref):
    members, rows, cells, block = fc_ref.shape
    total_rows = weight_ref.shape[0] // subcells
    slot = 128
    lanes = members * slot
    first = lax.axis_index("lat") * rows
    variables = cells // subcells
    cell_sub = lax.broadcasted_iota(jnp.int32, (cells, 1), 0) // variables
    pad = jnp.zeros((cells, slot - block), jnp.float32)
    for i in range(rows):
        g = first + i
        scale = jnp.zeros((cells, 1), jnp.float32)
        for s in range(subcells):
            scale = jnp.where(cell_sub == s, weight_ref[s * total_rows + g], scale)
        values = jnp.concatenate(
            [
                jnp.concatenate([fc_ref[n, i].astype(jnp.float32), pad], axis=1)
                for n in range(members)
            ],
            axis=1,
        )
        truth_slot = jnp.concatenate([truth_ref[i], pad], axis=1)
        truth = jnp.concatenate([truth_slot] * members, axis=1)
        spread = jnp.zeros((cells, lanes), jnp.float32)
        for k in range(1, (members + 1) // 2):
            term = softened_sign(values - pltpu.roll(values, k * slot, 1))
            spread = spread + term - pltpu.roll(term, lanes - k * slot, 1)
        if members % 2 == 0:
            spread = spread + softened_sign(
                values - pltpu.roll(values, (members // 2) * slot, 1)
            )
        grad = scale * (softened_sign(values - truth) - spread / members)
        coarse = None
        for part in split3(grad):
            term = jnp.dot(sub_t_ref[...], part, preferred_element_type=jnp.float32)
            coarse = term if coarse is None else coarse + term
        coarse = coarse.astype(out_ref.dtype)
        for m in range(members):
            out_ref[m, i] = coarse[:, m * slot : m * slot + block]


def grad_filtered_kernel(gc_ref, slope_ref, proj_t_ref, out_ref):
    blocks, rows = gc_ref.shape[0], gc_ref.shape[1]
    width_p = slope_ref.shape[2]
    for i in range(rows):
        row = jnp.concatenate([gc_ref[q, i] for q in range(blocks)], axis=1)
        width = row.shape[1]
        extra = width_p - width
        lo = extra // 2
        hi = extra - lo
        ring = jnp.concatenate([row, row[:, :lo], row[:, width - hi :]], axis=1)
        grad_act = jnp.dot(proj_t_ref[...], ring, preferred_element_type=jnp.float32)
        out_ref[i] = (grad_act * slope_ref[i]).astype(jnp.bfloat16)


def backward_terms(basis_ref, step_ref, quad_ref, table_ref, rows, sources, acc):
    total_rows = step_ref.shape[0]
    first = lax.axis_index("lat") * rows
    for e, src_ref, r in sources:
        cp, width_p = src_ref.shape[1], src_ref.shape[2]
        a_lo = max(0, 2 * HALF - e)
        a_hi = min(TAPS - 1, rows - 1 + 2 * HALF - e)
        if a_lo > a_hi:
            continue
        g = jnp.clip(first - HALF + e, 0, total_rows - 1)
        step = step_ref[g]
        weights = jnp.concatenate(
            [
                jnp.concatenate(
                    [table_ref[1, basis_ref[g * TAPS * TAPS + a * TAPS + b]] for b in range(TAPS)],
                    axis=1,
                )
                for a in range(a_lo, a_hi + 1)
            ],
            axis=0,
        )
        source = src_ref[r]
        rolled = []
        for b in range(TAPS):
            if b == HALF:
                rolled.append(source)
            else:
                shift = lax.rem((b - HALF) * step + width_p, width_p)
                rolled.append(pltpu.roll(source, shift, 1))
        stacked = jnp.concatenate(rolled, axis=0)
        part = jnp.dot(weights, stacked, preferred_element_type=jnp.float32)
        scale = quad_ref[g]
        for a in range(a_lo, a_hi + 1):
            i2 = e + a - 2 * HALF
            piece = part[(a - a_lo) * cp : (a - a_lo + 1) * cp] * scale
            acc[i2] = piece if acc[i2] is None else acc[i2] + piece
    return acc


def backward_own_kernel(basis_ref, step_ref, quad_ref, own_ref, table_ref, acc_ref):
    rows = own_ref.shape[0]
    acc = backward_terms(
        basis_ref, step_ref, quad_ref, table_ref, rows,
        [(HALF + r, own_ref, r) for r in range(rows)], [None] * rows,
    )
    for i2 in range(rows):
        acc_ref[i2] = acc[i2]


def backward_halo_kernel(basis_ref, step_ref, quad_ref, prev_ref, next_ref, acc_in_ref,
                         table_ref, out_ref):
    rows = acc_in_ref.shape[0]
    channels, width = out_ref.shape[1], out_ref.shape[2]
    acc = backward_terms(
        basis_ref, step_ref, quad_ref, table_ref, rows,
        [(e, prev_ref, e) for e in range(HALF)]
        + [(HALF + rows + e, next_ref, e) for e in range(HALF)],
        [acc_in_ref[i2] for i2 in range(rows)],
    )
    for i2 in range(rows):
        out_ref[i2] = acc[i2][:channels, :width].astype(out_ref.dtype)


def vmem():
    return pl.BlockSpec(memory_space=pltpu.VMEM)


def smem():
    return pl.BlockSpec(memory_space=pltpu.SMEM)


def on_device(latents, filters, project, subcell_maps, verifying_truth, basis_rows, step_rows):
    rows = latents.shape[1]
    channels = latents.shape[2]
    width = latents.shape[3]
    variables = project.shape[0]
    subcells = subcell_maps.shape[0]
    cp = round_up(channels, 16)
    vp = round_up(variables, 16)
    svp = subcells * variables
    width_p = ring_width(width)
    total_rows = rows * lax.axis_size("lat")
    first = lax.axis_index("lat") * rows

    quad_all = latitude_rows(total_rows, total_rows)
    weight_all = subcell_weight(0, total_rows, total_rows).reshape(-1)
    sub_t = pad_axis(subcell_maps.reshape(subcells * variables, variables).T, 0, vp)
    blocks = lax.axis_size("member")
    block = width // blocks
    truth = verifying_truth.reshape(subcells * variables, rows, block).transpose(1, 0, 2)

    table = jnp.concatenate([filters, jnp.zeros((1,) + filters.shape[1:], filters.dtype)], 0)
    table = pad_axis(pad_axis(table, 1, cp), 2, cp)
    tables = jnp.stack([table, table.transpose(0, 2, 1)])
    basis_flat = basis_rows.reshape(-1)

    proj_p = pad_axis(pad_axis(project, 0, vp), 1, cp)
    sub_p = pad_axis(pad_axis(subcell_maps.reshape(subcells * variables, variables), 0, svp), 1, vp)

    own = to_ring(pad_axis(latents[0], 1, cp), width_p)
    low, high = halo(own, "lat", HALF)

    own_part = pl.pallas_call(
        forward_own_kernel,
        out_shape=jax.ShapeDtypeStruct((rows, cp, width_p), jnp.float32),
        in_specs=[smem(), smem()] + [vmem()] * 2,
        out_specs=vmem(),
        cost_estimate=pl.CostEstimate(
            flops=2 * rows * TAPS * cp * rows * cp * width_p,
            transcendentals=0,
            bytes_accessed=rows * cp * width_p * 6,
        ),
    )(basis_flat, step_rows, own, tables)
    slope, fc = pl.pallas_call(
        forward_kernel,
        out_shape=(
            jax.ShapeDtypeStruct((rows, cp, width_p), jnp.float32),
            jax.ShapeDtypeStruct((blocks, rows, svp, block), jnp.bfloat16),
        ),
        in_specs=[smem(), smem(), smem()] + [vmem()] * 6,
        out_specs=(vmem(), vmem()),
    )(basis_flat, step_rows, quad_all, low, high, own_part, tables, proj_p, sub_p)

    fc_owned = lax.all_to_all(fc, "member", split_axis=0, concat_axis=0, tiled=True)
    gc_owned = pl.pallas_call(
        functools.partial(score_kernel, subcells),
        out_shape=jax.ShapeDtypeStruct((blocks, rows, vp, block), jnp.bfloat16),
        in_specs=[smem()] + [vmem()] * 3,
        out_specs=vmem(),
    )(weight_all, sub_t, fc_owned, truth)
    gc_home = lax.all_to_all(gc_owned, "member", split_axis=0, concat_axis=0, tiled=True)
    proj_t = pad_axis(pad_axis(project.T, 0, cp), 1, vp)
    grad_filtered = pl.pallas_call(
        grad_filtered_kernel,
        out_shape=jax.ShapeDtypeStruct((rows, cp, width_p), jnp.bfloat16),
        in_specs=[vmem()] * 3,
        out_specs=vmem(),
    )(gc_home, slope, proj_t)

    g_low, g_high = halo(grad_filtered, "lat", HALF)
    own_terms = pl.pallas_call(
        backward_own_kernel,
        out_shape=jax.ShapeDtypeStruct((rows, cp, width_p), jnp.float32),
        in_specs=[smem(), smem(), smem()] + [vmem()] * 2,
        out_specs=vmem(),
        cost_estimate=pl.CostEstimate(
            flops=2 * rows * rows * cp * TAPS * cp * width_p,
            transcendentals=0,
            bytes_accessed=rows * cp * width_p * 6,
        ),
    )(basis_flat, step_rows, quad_all, grad_filtered, tables)
    result = pl.pallas_call(
        backward_halo_kernel,
        out_shape=jax.ShapeDtypeStruct((rows, channels, width), jnp.bfloat16),
        in_specs=[smem(), smem(), smem()] + [vmem()] * 4,
        out_specs=vmem(),
    )(basis_flat, step_rows, quad_all, g_low, g_high, own_terms, tables)
    return result[None]


def solution(mesh):
    placed = (
        P("member", "lat", None, None),
        P(),
        P(),
        P(),
        P(None, None, "lat", "member"),
        P(),
        P(),
    )
    return jax.shard_map(
        on_device,
        mesh=mesh,
        in_specs=placed,
        out_specs=P("member", "lat", None, None),
        check_vma=False,
    )
```

```python
import functools

import jax
import jax.numpy as jnp
from jax import lax
from jax.experimental import pallas as pl
from jax.experimental.pallas import tpu as pltpu
from jax.sharding import PartitionSpec as P

TAPS = 7
HALF = 3
MAX_STEP = 3


def round_up(value, unit):
    return (value + unit - 1) // unit * unit


def ring_width(width):
    return round_up(width + 4 * HALF * MAX_STEP + 2, 128)


def to_ring(block, width_p):
    width = block.shape[-1]
    extra = width_p - width
    lo = extra // 2
    hi = extra - lo
    return jnp.concatenate(
        [block, block[..., :lo], block[..., width - hi :]], axis=-1
    )


def pad_axis(block, axis, size):
    pads = [(0, 0)] * block.ndim
    pads[axis] = (0, size - block.shape[axis])
    return jnp.pad(block, pads)


def halo(block, axis_name, width):
    count = lax.axis_size(axis_name)
    forward = [(i, i + 1) for i in range(count - 1)]
    backward = [(target, source) for source, target in forward]
    low = lax.ppermute(block[block.shape[0] - width :], axis_name, forward)
    high = lax.ppermute(block[:width], axis_name, backward)
    return low, high


def latitude_rows(count, total):
    rows = jnp.arange(count, dtype=jnp.int32).astype(jnp.float32)
    return jnp.cos(((rows + 0.5) / total - 0.5) * jnp.pi)


def subcell_weight(first, count, total):
    rows = (first + jnp.arange(count, dtype=jnp.int32)).astype(jnp.float32)
    sub_row = jnp.array([0.0, 0.0, 1.0, 1.0], jnp.float32)
    fine = 2.0 * rows[None, :] + sub_row[:, None]
    return jnp.cos(((fine + 0.5) / (2.0 * total) - 0.5) * jnp.pi)


def softened_sign(diff):
    return diff / jnp.sqrt(diff * diff + 0.01)


SQRT_2_OVER_PI = 0.7978845608028654


def gelu(x):
    inner = SQRT_2_OVER_PI * (x + 0.044715 * (x * x * x))
    return x * (0.5 * (1.0 + jnp.tanh(inner)))


def gelu_grad(x):
    inner = SQRT_2_OVER_PI * (x + 0.044715 * (x * x * x))
    t = jnp.tanh(inner)
    d_inner = SQRT_2_OVER_PI * (1.0 + 3.0 * 0.044715 * (x * x))
    return 0.5 * (1.0 + t) + x * (0.5 * (1.0 - t * t)) * d_inner


def gelu_and_grad(x):
    inner = SQRT_2_OVER_PI * (x + 0.044715 * (x * x * x))
    t = jnp.tanh(inner)
    d_inner = SQRT_2_OVER_PI * (1.0 + 3.0 * 0.044715 * (x * x))
    half = 0.5 * (1.0 + t)
    return x * half, half + x * (0.5 * (1.0 - t * t)) * d_inner


def forward_kernel(basis_ref, step_ref, quad_ref, prev_ref, own_ref, next_ref, table_ref,
                   proj_ref, sub_ref, slope_ref, fc_ref):
    rows, cp, width_p = own_ref.shape
    first = lax.axis_index("lat") * rows
    ext = (
        [prev_ref[e] for e in range(HALF)]
        + [own_ref[e] for e in range(rows)]
        + [next_ref[e] for e in range(HALF)]
    )
    for i in range(rows):
        g = first + i
        step = step_ref[g]
        weights = jnp.concatenate(
            [
                jnp.concatenate(
                    [table_ref[0, basis_ref[g * TAPS * TAPS + a * TAPS + b]] for a in range(TAPS)],
                    axis=1,
                )
                for b in range(TAPS)
            ],
            axis=0,
        )
        stacked = jnp.concatenate(ext[i : i + TAPS], axis=0)
        taps = jnp.dot(weights, stacked, preferred_element_type=jnp.float32)
        total = taps[HALF * cp : (HALF + 1) * cp]
        for b in range(TAPS):
            if b == HALF:
                continue
            shift = lax.rem((HALF - b) * step + width_p, width_p)
            total = total + pltpu.roll(taps[b * cp : (b + 1) * cp], shift, 1)
        filtered = total * quad_ref[g]
        gelu_value, gelu_slope = gelu_and_grad(filtered)
        slope_ref[i] = gelu_slope
        activated = gelu_value.astype(jnp.bfloat16)
        coarse = jnp.dot(
            proj_ref[...], activated, preferred_element_type=jnp.float32
        ).astype(jnp.bfloat16)
        forecast = jnp.dot(
            sub_ref[...], coarse, preferred_element_type=jnp.float32
        ).astype(jnp.bfloat16)
        blocks, block = fc_ref.shape[0], fc_ref.shape[3]
        for q in range(blocks):
            fc_ref[q, i] = forecast[:, q * block : (q + 1) * block]


def split3(x):
    hi = x.astype(jnp.bfloat16)
    rest = x - hi.astype(jnp.float32)
    mid = rest.astype(jnp.bfloat16)
    lo = (rest - mid.astype(jnp.float32)).astype(jnp.bfloat16)
    return hi, mid, lo


def score_kernel(subcells, weight_ref, sub_t_ref, fc_ref, truth_ref, out_ref):
    members, rows, cells, block = fc_ref.shape
    total_rows = weight_ref.shape[0] // subcells
    slot = 128
    lanes = members * slot
    first = lax.axis_index("lat") * rows
    variables = cells // subcells
    cell_sub = lax.broadcasted_iota(jnp.int32, (cells, 1), 0) // variables
    pad = jnp.zeros((cells, slot - block), jnp.float32)
    for i in range(rows):
        g = first + i
        scale = jnp.zeros((cells, 1), jnp.float32)
        for s in range(subcells):
            scale = jnp.where(cell_sub == s, weight_ref[s * total_rows + g], scale)
        values = jnp.concatenate(
            [
                jnp.concatenate([fc_ref[n, i].astype(jnp.float32), pad], axis=1)
                for n in range(members)
            ],
            axis=1,
        )
        truth_slot = jnp.concatenate([truth_ref[i], pad], axis=1)
        truth = jnp.concatenate([truth_slot] * members, axis=1)
        spread = jnp.zeros((cells, lanes), jnp.float32)
        for k in range(1, (members + 1) // 2):
            term = softened_sign(values - pltpu.roll(values, k * slot, 1))
            spread = spread + term - pltpu.roll(term, lanes - k * slot, 1)
        if members % 2 == 0:
            spread = spread + softened_sign(
                values - pltpu.roll(values, (members // 2) * slot, 1)
            )
        grad = scale * (softened_sign(values - truth) - spread / members)
        coarse = None
        for part in split3(grad):
            term = jnp.dot(sub_t_ref[...], part, preferred_element_type=jnp.float32)
            coarse = term if coarse is None else coarse + term
        coarse = coarse.astype(out_ref.dtype)
        for m in range(members):
            out_ref[m, i] = coarse[:, m * slot : m * slot + block]


def grad_filtered_kernel(gc_ref, slope_ref, proj_t_ref, out_ref):
    blocks, rows = gc_ref.shape[0], gc_ref.shape[1]
    width_p = slope_ref.shape[2]
    for i in range(rows):
        row = jnp.concatenate([gc_ref[q, i] for q in range(blocks)], axis=1)
        width = row.shape[1]
        extra = width_p - width
        lo = extra // 2
        hi = extra - lo
        ring = jnp.concatenate([row, row[:, :lo], row[:, width - hi :]], axis=1)
        grad_act = jnp.dot(
            proj_t_ref[...], ring.astype(jnp.float32), preferred_element_type=jnp.float32
        )
        out_ref[i] = (grad_act * slope_ref[i]).astype(jnp.bfloat16)


def backward_terms(basis_ref, step_ref, quad_ref, table_ref, rows, sources, acc):
    total_rows = step_ref.shape[0]
    first = lax.axis_index("lat") * rows
    for e, src_ref, r in sources:
        cp, width_p = src_ref.shape[1], src_ref.shape[2]
        a_lo = max(0, 2 * HALF - e)
        a_hi = min(TAPS - 1, rows - 1 + 2 * HALF - e)
        if a_lo > a_hi:
            continue
        g = jnp.clip(first - HALF + e, 0, total_rows - 1)
        step = step_ref[g]
        weights = jnp.concatenate(
            [
                jnp.concatenate(
                    [table_ref[1, basis_ref[g * TAPS * TAPS + a * TAPS + b]] for b in range(TAPS)],
                    axis=1,
                )
                for a in range(a_lo, a_hi + 1)
            ],
            axis=0,
        )
        source = src_ref[r]
        rolled = []
        for b in range(TAPS):
            if b == HALF:
                rolled.append(source)
            else:
                shift = lax.rem((b - HALF) * step + width_p, width_p)
                rolled.append(pltpu.roll(source, shift, 1))
        stacked = jnp.concatenate(rolled, axis=0)
        part = jnp.dot(weights, stacked, preferred_element_type=jnp.float32)
        scale = quad_ref[g]
        for a in range(a_lo, a_hi + 1):
            i2 = e + a - 2 * HALF
            piece = part[(a - a_lo) * cp : (a - a_lo + 1) * cp] * scale
            acc[i2] = piece if acc[i2] is None else acc[i2] + piece
    return acc


def backward_own_kernel(basis_ref, step_ref, quad_ref, own_ref, table_ref, acc_ref):
    rows = own_ref.shape[0]
    acc = backward_terms(
        basis_ref, step_ref, quad_ref, table_ref, rows,
        [(HALF + r, own_ref, r) for r in range(rows)], [None] * rows,
    )
    for i2 in range(rows):
        acc_ref[i2] = acc[i2]


def backward_halo_kernel(basis_ref, step_ref, quad_ref, prev_ref, next_ref, acc_in_ref,
                         table_ref, out_ref):
    rows = acc_in_ref.shape[0]
    channels, width = out_ref.shape[1], out_ref.shape[2]
    acc = backward_terms(
        basis_ref, step_ref, quad_ref, table_ref, rows,
        [(e, prev_ref, e) for e in range(HALF)]
        + [(HALF + rows + e, next_ref, e) for e in range(HALF)],
        [acc_in_ref[i2] for i2 in range(rows)],
    )
    for i2 in range(rows):
        out_ref[i2] = acc[i2][:channels, :width].astype(out_ref.dtype)


def vmem():
    return pl.BlockSpec(memory_space=pltpu.VMEM)


def smem():
    return pl.BlockSpec(memory_space=pltpu.SMEM)


def on_device(latents, filters, project, subcell_maps, verifying_truth, basis_rows, step_rows):
    rows = latents.shape[1]
    channels = latents.shape[2]
    width = latents.shape[3]
    variables = project.shape[0]
    subcells = subcell_maps.shape[0]
    cp = round_up(channels, 16)
    vp = round_up(variables, 16)
    svp = subcells * variables
    width_p = ring_width(width)
    total_rows = rows * lax.axis_size("lat")
    first = lax.axis_index("lat") * rows

    quad_all = latitude_rows(total_rows, total_rows)
    weight_all = subcell_weight(0, total_rows, total_rows).reshape(-1)
    vq = round_up(variables, 8)
    sub_t = pad_axis(subcell_maps.reshape(subcells * variables, variables).T, 0, vq)
    blocks = lax.axis_size("member")
    block = width // blocks
    truth = verifying_truth.reshape(subcells * variables, rows, block).transpose(1, 0, 2)

    table = jnp.concatenate([filters, jnp.zeros((1,) + filters.shape[1:], filters.dtype)], 0)
    table = pad_axis(pad_axis(table, 1, cp), 2, cp)
    tables = jnp.stack([table, table.transpose(0, 2, 1)])
    basis_flat = basis_rows.reshape(-1)

    proj_p = pad_axis(pad_axis(project, 0, vp), 1, cp)
    sub_p = pad_axis(pad_axis(subcell_maps.reshape(subcells * variables, variables), 0, svp), 1, vp)

    own = to_ring(pad_axis(latents[0], 1, cp), width_p)
    low, high = halo(own, "lat", HALF)

    slope, fc = pl.pallas_call(
        forward_kernel,
        out_shape=(
            jax.ShapeDtypeStruct((rows, cp, width_p), jnp.float32),
            jax.ShapeDtypeStruct((blocks, rows, svp, block), jnp.bfloat16),
        ),
        in_specs=[smem(), smem(), smem()] + [vmem()] * 6,
        out_specs=(vmem(), vmem()),
    )(basis_flat, step_rows, quad_all, low, own, high, tables, proj_p, sub_p)

    fc_owned = lax.all_to_all(fc, "member", split_axis=0, concat_axis=0, tiled=True)
    gc_owned = pl.pallas_call(
        functools.partial(score_kernel, subcells),
        out_shape=jax.ShapeDtypeStruct((blocks, rows, vq, block), jnp.bfloat16),
        in_specs=[smem()] + [vmem()] * 3,
        out_specs=vmem(),
    )(weight_all, sub_t, fc_owned, truth)
    gc_home = lax.all_to_all(gc_owned, "member", split_axis=0, concat_axis=0, tiled=True)
    proj_t = pad_axis(pad_axis(project.T, 0, cp), 1, vq).astype(jnp.float32)
    grad_filtered = pl.pallas_call(
        grad_filtered_kernel,
        out_shape=jax.ShapeDtypeStruct((rows, cp, width_p), jnp.bfloat16),
        in_specs=[vmem()] * 3,
        out_specs=vmem(),
    )(gc_home, slope, proj_t)

    g_low, g_high = halo(grad_filtered, "lat", HALF)
    own_terms = pl.pallas_call(
        backward_own_kernel,
        out_shape=jax.ShapeDtypeStruct((rows, cp, width_p), jnp.float32),
        in_specs=[smem(), smem(), smem()] + [vmem()] * 2,
        out_specs=vmem(),
        cost_estimate=pl.CostEstimate(
            flops=2 * rows * rows * cp * TAPS * cp * width_p,
            transcendentals=0,
            bytes_accessed=rows * cp * width_p * 6,
        ),
    )(basis_flat, step_rows, quad_all, grad_filtered, tables)
    result = pl.pallas_call(
        backward_halo_kernel,
        out_shape=jax.ShapeDtypeStruct((rows, channels, width), jnp.bfloat16),
        in_specs=[smem(), smem(), smem()] + [vmem()] * 4,
        out_specs=vmem(),
    )(basis_flat, step_rows, quad_all, g_low, g_high, own_terms, tables)
    return result[None]


def solution(mesh):
    placed = (
        P("member", "lat", None, None),
        P(),
        P(),
        P(),
        P(None, None, "lat", "member"),
        P(),
        P(),
    )
    return jax.shard_map(
        on_device,
        mesh=mesh,
        in_specs=placed,
        out_specs=P("member", "lat", None, None),
        check_vma=False,
    )
```

```python
import functools

import jax
import jax.numpy as jnp
from jax import lax
from jax.experimental import pallas as pl
from jax.experimental.pallas import tpu as pltpu
from jax.sharding import PartitionSpec as P

TAPS = 7
HALF = 3
MAX_STEP = 3


def round_up(value, unit):
    return (value + unit - 1) // unit * unit


def ring_width(width):
    return round_up(width + 4 * HALF * MAX_STEP + 2, 128)


def to_ring(block, width_p):
    width = block.shape[-1]
    extra = width_p - width
    lo = extra // 2
    hi = extra - lo
    return jnp.concatenate(
        [block, block[..., :lo], block[..., width - hi :]], axis=-1
    )


def pad_axis(block, axis, size):
    pads = [(0, 0)] * block.ndim
    pads[axis] = (0, size - block.shape[axis])
    return jnp.pad(block, pads)


def halo(block, axis_name, width):
    count = lax.axis_size(axis_name)
    forward = [(i, i + 1) for i in range(count - 1)]
    backward = [(target, source) for source, target in forward]
    low = lax.ppermute(block[block.shape[0] - width :], axis_name, forward)
    high = lax.ppermute(block[:width], axis_name, backward)
    return low, high


def latitude_rows(count, total):
    rows = jnp.arange(count, dtype=jnp.int32).astype(jnp.float32)
    return jnp.cos(((rows + 0.5) / total - 0.5) * jnp.pi)


def subcell_weight(first, count, total):
    rows = (first + jnp.arange(count, dtype=jnp.int32)).astype(jnp.float32)
    sub_row = jnp.array([0.0, 0.0, 1.0, 1.0], jnp.float32)
    fine = 2.0 * rows[None, :] + sub_row[:, None]
    return jnp.cos(((fine + 0.5) / (2.0 * total) - 0.5) * jnp.pi)


def softened_sign(diff):
    return diff / jnp.sqrt(diff * diff + 0.01)


SQRT_2_OVER_PI = 0.7978845608028654


def gelu(x):
    inner = SQRT_2_OVER_PI * (x + 0.044715 * (x * x * x))
    return x * (0.5 * (1.0 + jnp.tanh(inner)))


def gelu_grad(x):
    inner = SQRT_2_OVER_PI * (x + 0.044715 * (x * x * x))
    t = jnp.tanh(inner)
    d_inner = SQRT_2_OVER_PI * (1.0 + 3.0 * 0.044715 * (x * x))
    return 0.5 * (1.0 + t) + x * (0.5 * (1.0 - t * t)) * d_inner


def gelu_and_grad(x):
    inner = SQRT_2_OVER_PI * (x + 0.044715 * (x * x * x))
    t = jnp.tanh(inner)
    d_inner = SQRT_2_OVER_PI * (1.0 + 3.0 * 0.044715 * (x * x))
    half = 0.5 * (1.0 + t)
    return x * half, half + x * (0.5 * (1.0 - t * t)) * d_inner


def forward_kernel(basis_ref, step_ref, quad_ref, prev_ref, own_ref, next_ref, table_ref,
                   proj_ref, sub_ref, slope_ref, fc_ref):
    rows, cp, width_p = own_ref.shape
    first = lax.axis_index("lat") * rows
    ext = (
        [prev_ref[e] for e in range(HALF)]
        + [own_ref[e] for e in range(rows)]
        + [next_ref[e] for e in range(HALF)]
    )
    for i in range(rows):
        g = first + i
        step = step_ref[g]
        weights = jnp.concatenate(
            [
                jnp.concatenate(
                    [table_ref[0, basis_ref[g * TAPS * TAPS + a * TAPS + b]] for a in range(TAPS)],
                    axis=1,
                )
                for b in range(TAPS)
            ],
            axis=0,
        )
        stacked = jnp.concatenate(ext[i : i + TAPS], axis=0)
        taps = jnp.dot(weights, stacked, preferred_element_type=jnp.float32)
        total = taps[HALF * cp : (HALF + 1) * cp]
        for b in range(TAPS):
            if b == HALF:
                continue
            shift = lax.rem((HALF - b) * step + width_p, width_p)
            total = total + pltpu.roll(taps[b * cp : (b + 1) * cp], shift, 1)
        filtered = total * quad_ref[g]
        gelu_value, gelu_slope = gelu_and_grad(filtered)
        slope_ref[i] = gelu_slope
        activated = gelu_value.astype(jnp.bfloat16)
        coarse = jnp.dot(
            proj_ref[...], activated, preferred_element_type=jnp.float32
        ).astype(jnp.bfloat16)
        forecast = jnp.dot(
            sub_ref[...], coarse, preferred_element_type=jnp.float32
        ).astype(jnp.bfloat16)
        blocks, block = fc_ref.shape[0], fc_ref.shape[3]
        for q in range(blocks):
            fc_ref[q, i] = forecast[:, q * block : (q + 1) * block]


def split3(x):
    hi = x.astype(jnp.bfloat16)
    rest = x - hi.astype(jnp.float32)
    mid = rest.astype(jnp.bfloat16)
    lo = (rest - mid.astype(jnp.float32)).astype(jnp.bfloat16)
    return hi, mid, lo


def score_kernel(subcells, weight_ref, sub_t_ref, fc_ref, truth_ref, out_ref):
    members, rows, cells, block = fc_ref.shape
    total_rows = weight_ref.shape[0] // subcells
    slot = 128
    lanes = members * slot
    first = lax.axis_index("lat") * rows
    variables = cells // subcells
    cell_sub = lax.broadcasted_iota(jnp.int32, (cells, 1), 0) // variables
    pad = jnp.zeros((cells, slot - block), jnp.float32)
    for i in range(rows):
        g = first + i
        scale = jnp.zeros((cells, 1), jnp.float32)
        for s in range(subcells):
            scale = jnp.where(cell_sub == s, weight_ref[s * total_rows + g], scale)
        values = jnp.concatenate(
            [
                jnp.concatenate([fc_ref[n, i].astype(jnp.float32), pad], axis=1)
                for n in range(members)
            ],
            axis=1,
        )
        truth_slot = jnp.concatenate([truth_ref[i], pad], axis=1)
        truth = jnp.concatenate([truth_slot] * members, axis=1)
        spread = jnp.zeros((cells, lanes), jnp.float32)
        for k in range(1, (members + 1) // 2):
            term = softened_sign(values - pltpu.roll(values, k * slot, 1))
            spread = spread + term - pltpu.roll(term, lanes - k * slot, 1)
        if members % 2 == 0:
            spread = spread + softened_sign(
                values - pltpu.roll(values, (members // 2) * slot, 1)
            )
        grad = scale * (softened_sign(values - truth) - spread / members)
        coarse = None
        for part in split3(grad):
            term = jnp.dot(sub_t_ref[...], part, preferred_element_type=jnp.float32)
            coarse = term if coarse is None else coarse + term
        coarse = coarse.astype(out_ref.dtype)
        for m in range(members):
            out_ref[m, i] = coarse[:, m * slot : m * slot + block]


def grad_filtered_kernel(gc_ref, slope_ref, proj_t_ref, out_ref):
    blocks, rows = gc_ref.shape[0], gc_ref.shape[1]
    width_p = slope_ref.shape[2]
    for i in range(rows):
        row = jnp.concatenate([gc_ref[q, i] for q in range(blocks)], axis=1)
        width = row.shape[1]
        extra = width_p - width
        lo = extra // 2
        hi = extra - lo
        ring = jnp.concatenate([row, row[:, :lo], row[:, width - hi :]], axis=1)
        grad_act = jnp.dot(
            proj_t_ref[...], ring.astype(jnp.float32), preferred_element_type=jnp.float32
        )
        out_ref[i] = (grad_act * slope_ref[i]).astype(jnp.bfloat16)


def backward_terms(basis_ref, step_ref, quad_ref, table_ref, rows, sources, acc):
    total_rows = step_ref.shape[0]
    first = lax.axis_index("lat") * rows
    for e, src_ref, r in sources:
        cp, width_p = src_ref.shape[1], src_ref.shape[2]
        a_lo = max(0, 2 * HALF - e)
        a_hi = min(TAPS - 1, rows - 1 + 2 * HALF - e)
        if a_lo > a_hi:
            continue
        g = jnp.clip(first - HALF + e, 0, total_rows - 1)
        step = step_ref[g]
        weights = jnp.concatenate(
            [
                jnp.concatenate(
                    [table_ref[1, basis_ref[g * TAPS * TAPS + a * TAPS + b]] for b in range(TAPS)],
                    axis=1,
                )
                for a in range(a_lo, a_hi + 1)
            ],
            axis=0,
        )
        source = src_ref[r]
        rolled = []
        for b in range(TAPS):
            if b == HALF:
                rolled.append(source)
            else:
                shift = lax.rem((b - HALF) * step + width_p, width_p)
                rolled.append(pltpu.roll(source, shift, 1))
        stacked = jnp.concatenate(rolled, axis=0)
        part = jnp.dot(weights, stacked, preferred_element_type=jnp.float32)
        scale = quad_ref[g]
        for a in range(a_lo, a_hi + 1):
            i2 = e + a - 2 * HALF
            piece = part[(a - a_lo) * cp : (a - a_lo + 1) * cp] * scale
            acc[i2] = piece if acc[i2] is None else acc[i2] + piece
    return acc


def backward_own_kernel(basis_ref, step_ref, quad_ref, own_ref, table_ref, acc_ref):
    rows = own_ref.shape[0]
    acc = backward_terms(
        basis_ref, step_ref, quad_ref, table_ref, rows,
        [(HALF + r, own_ref, r) for r in range(rows)], [None] * rows,
    )
    for i2 in range(rows):
        acc_ref[i2] = acc[i2]


def backward_prev_kernel(basis_ref, step_ref, quad_ref, prev_ref, acc_in_ref, table_ref,
                         acc_ref):
    rows = acc_in_ref.shape[0]
    acc = backward_terms(
        basis_ref, step_ref, quad_ref, table_ref, rows,
        [(e, prev_ref, e) for e in range(HALF)],
        [acc_in_ref[i2] for i2 in range(rows)],
    )
    for i2 in range(rows):
        acc_ref[i2] = acc[i2]


def backward_next_kernel(basis_ref, step_ref, quad_ref, next_ref, acc_in_ref, table_ref,
                         out_ref):
    rows = acc_in_ref.shape[0]
    channels, width = out_ref.shape[1], out_ref.shape[2]
    acc = backward_terms(
        basis_ref, step_ref, quad_ref, table_ref, rows,
        [(HALF + rows + e, next_ref, e) for e in range(HALF)],
        [acc_in_ref[i2] for i2 in range(rows)],
    )
    for i2 in range(rows):
        out_ref[i2] = acc[i2][:channels, :width].astype(out_ref.dtype)


def vmem():
    return pl.BlockSpec(memory_space=pltpu.VMEM)


def smem():
    return pl.BlockSpec(memory_space=pltpu.SMEM)


def on_device(latents, filters, project, subcell_maps, verifying_truth, basis_rows, step_rows):
    rows = latents.shape[1]
    channels = latents.shape[2]
    width = latents.shape[3]
    variables = project.shape[0]
    subcells = subcell_maps.shape[0]
    cp = round_up(channels, 16)
    vp = round_up(variables, 16)
    svp = subcells * variables
    width_p = ring_width(width)
    total_rows = rows * lax.axis_size("lat")
    first = lax.axis_index("lat") * rows

    quad_all = latitude_rows(total_rows, total_rows)
    weight_all = subcell_weight(0, total_rows, total_rows).reshape(-1)
    vq = round_up(variables, 8)
    sub_t = pad_axis(subcell_maps.reshape(subcells * variables, variables).T, 0, vq)
    blocks = lax.axis_size("member")
    block = width // blocks
    truth = verifying_truth.reshape(subcells * variables, rows, block).transpose(1, 0, 2)

    table = jnp.concatenate([filters, jnp.zeros((1,) + filters.shape[1:], filters.dtype)], 0)
    table = pad_axis(pad_axis(table, 1, cp), 2, cp)
    tables = jnp.stack([table, table.transpose(0, 2, 1)])
    basis_flat = basis_rows.reshape(-1)

    proj_p = pad_axis(pad_axis(project, 0, vp), 1, cp)
    sub_p = pad_axis(pad_axis(subcell_maps.reshape(subcells * variables, variables), 0, svp), 1, vp)

    own = to_ring(pad_axis(latents[0], 1, cp), width_p)
    low, high = halo(own, "lat", HALF)

    slope, fc = pl.pallas_call(
        forward_kernel,
        out_shape=(
            jax.ShapeDtypeStruct((rows, cp, width_p), jnp.float32),
            jax.ShapeDtypeStruct((blocks, rows, svp, block), jnp.bfloat16),
        ),
        in_specs=[smem(), smem(), smem()] + [vmem()] * 6,
        out_specs=(vmem(), vmem()),
    )(basis_flat, step_rows, quad_all, low, own, high, tables, proj_p, sub_p)

    fc_owned = lax.all_to_all(fc, "member", split_axis=0, concat_axis=0, tiled=True)
    gc_owned = pl.pallas_call(
        functools.partial(score_kernel, subcells),
        out_shape=jax.ShapeDtypeStruct((blocks, rows, vq, block), jnp.bfloat16),
        in_specs=[smem()] + [vmem()] * 3,
        out_specs=vmem(),
    )(weight_all, sub_t, fc_owned, truth)
    gc_home = lax.all_to_all(gc_owned, "member", split_axis=0, concat_axis=0, tiled=True)
    proj_t = pad_axis(pad_axis(project.T, 0, cp), 1, vq).astype(jnp.float32)
    grad_filtered = pl.pallas_call(
        grad_filtered_kernel,
        out_shape=jax.ShapeDtypeStruct((rows, cp, width_p), jnp.bfloat16),
        in_specs=[vmem()] * 3,
        out_specs=vmem(),
    )(gc_home, slope, proj_t)

    g_low, g_high = halo(grad_filtered, "lat", HALF)
    own_terms = pl.pallas_call(
        backward_own_kernel,
        out_shape=jax.ShapeDtypeStruct((rows, cp, width_p), jnp.float32),
        in_specs=[smem(), smem(), smem()] + [vmem()] * 2,
        out_specs=vmem(),
        cost_estimate=pl.CostEstimate(
            flops=2 * rows * rows * cp * TAPS * cp * width_p,
            transcendentals=0,
            bytes_accessed=rows * cp * width_p * 6,
        ),
    )(basis_flat, step_rows, quad_all, grad_filtered, tables)
    with_prev = pl.pallas_call(
        backward_prev_kernel,
        out_shape=jax.ShapeDtypeStruct((rows, cp, width_p), jnp.float32),
        in_specs=[smem(), smem(), smem()] + [vmem()] * 3,
        out_specs=vmem(),
        cost_estimate=pl.CostEstimate(
            flops=2 * rows * HALF * cp * TAPS * cp * width_p,
            transcendentals=0,
            bytes_accessed=rows * cp * width_p * 10,
        ),
    )(basis_flat, step_rows, quad_all, g_low, own_terms, tables)
    result = pl.pallas_call(
        backward_next_kernel,
        out_shape=jax.ShapeDtypeStruct((rows, channels, width), jnp.bfloat16),
        in_specs=[smem(), smem(), smem()] + [vmem()] * 3,
        out_specs=vmem(),
    )(basis_flat, step_rows, quad_all, g_high, with_prev, tables)
    return result[None]


def solution(mesh):
    placed = (
        P("member", "lat", None, None),
        P(),
        P(),
        P(),
        P(None, None, "lat", "member"),
        P(),
        P(),
    )
    return jax.shard_map(
        on_device,
        mesh=mesh,
        in_specs=placed,
        out_specs=P("member", "lat", None, None),
        check_vma=False,
    )
```

```python
import functools

import jax
import jax.numpy as jnp
from jax import lax
from jax.experimental import pallas as pl
from jax.experimental.pallas import tpu as pltpu
from jax.sharding import PartitionSpec as P

TAPS = 7
HALF = 3
MAX_STEP = 3


def round_up(value, unit):
    return (value + unit - 1) // unit * unit


def ring_width(width):
    return round_up(width + 4 * HALF * MAX_STEP + 2, 128)


def to_ring(block, width_p):
    width = block.shape[-1]
    extra = width_p - width
    lo = extra // 2
    hi = extra - lo
    return jnp.concatenate(
        [block, block[..., :lo], block[..., width - hi :]], axis=-1
    )


def pad_axis(block, axis, size):
    pads = [(0, 0)] * block.ndim
    pads[axis] = (0, size - block.shape[axis])
    return jnp.pad(block, pads)


def halo(block, axis_name, width):
    count = lax.axis_size(axis_name)
    forward = [(i, i + 1) for i in range(count - 1)]
    backward = [(target, source) for source, target in forward]
    low = lax.ppermute(block[block.shape[0] - width :], axis_name, forward)
    high = lax.ppermute(block[:width], axis_name, backward)
    return low, high


def latitude_rows(count, total):
    rows = jnp.arange(count, dtype=jnp.int32).astype(jnp.float32)
    return jnp.cos(((rows + 0.5) / total - 0.5) * jnp.pi)


def subcell_weight(first, count, total):
    rows = (first + jnp.arange(count, dtype=jnp.int32)).astype(jnp.float32)
    sub_row = jnp.array([0.0, 0.0, 1.0, 1.0], jnp.float32)
    fine = 2.0 * rows[None, :] + sub_row[:, None]
    return jnp.cos(((fine + 0.5) / (2.0 * total) - 0.5) * jnp.pi)


def softened_sign(diff):
    return diff / jnp.sqrt(diff * diff + 0.01)


SQRT_2_OVER_PI = 0.7978845608028654


def gelu(x):
    inner = SQRT_2_OVER_PI * (x + 0.044715 * (x * x * x))
    return x * (0.5 * (1.0 + jnp.tanh(inner)))


def gelu_grad(x):
    inner = SQRT_2_OVER_PI * (x + 0.044715 * (x * x * x))
    t = jnp.tanh(inner)
    d_inner = SQRT_2_OVER_PI * (1.0 + 3.0 * 0.044715 * (x * x))
    return 0.5 * (1.0 + t) + x * (0.5 * (1.0 - t * t)) * d_inner


def gelu_and_grad(x):
    inner = SQRT_2_OVER_PI * (x + 0.044715 * (x * x * x))
    t = jnp.tanh(inner)
    d_inner = SQRT_2_OVER_PI * (1.0 + 3.0 * 0.044715 * (x * x))
    half = 0.5 * (1.0 + t)
    return x * half, half + x * (0.5 * (1.0 - t * t)) * d_inner


def forward_kernel(basis_ref, step_ref, quad_ref, prev_ref, own_ref, next_ref, table_ref,
                   proj_ref, sub_ref, slope_ref, fc_ref):
    rows, cp, width_p = own_ref.shape
    first = lax.axis_index("lat") * rows
    ext = (
        [prev_ref[e] for e in range(HALF)]
        + [own_ref[e] for e in range(rows)]
        + [next_ref[e] for e in range(HALF)]
    )
    for i in range(rows):
        g = first + i
        step = step_ref[g]
        weights = jnp.concatenate(
            [
                jnp.concatenate(
                    [table_ref[0, basis_ref[g * TAPS * TAPS + a * TAPS + b]] for a in range(TAPS)],
                    axis=1,
                )
                for b in range(TAPS)
            ],
            axis=0,
        )
        stacked = jnp.concatenate(ext[i : i + TAPS], axis=0)
        taps = jnp.dot(weights, stacked, preferred_element_type=jnp.float32)
        total = taps[HALF * cp : (HALF + 1) * cp]
        for b in range(TAPS):
            if b == HALF:
                continue
            shift = lax.rem((HALF - b) * step + width_p, width_p)
            total = total + pltpu.roll(taps[b * cp : (b + 1) * cp], shift, 1)
        filtered = total * quad_ref[g]
        gelu_value, gelu_slope = gelu_and_grad(filtered)
        slope_ref[i] = gelu_slope
        activated = gelu_value.astype(jnp.bfloat16)
        coarse = jnp.dot(
            proj_ref[...], activated, preferred_element_type=jnp.float32
        ).astype(jnp.bfloat16)
        forecast = jnp.dot(
            sub_ref[...], coarse, preferred_element_type=jnp.float32
        ).astype(jnp.bfloat16)
        blocks, block = fc_ref.shape[0], fc_ref.shape[2]
        cells = forecast.shape[0]
        for q in range(blocks):
            fc_ref[q, i * cells : (i + 1) * cells] = forecast[:, q * block : (q + 1) * block]


def split3(x):
    hi = x.astype(jnp.bfloat16)
    rest = x - hi.astype(jnp.float32)
    mid = rest.astype(jnp.bfloat16)
    lo = (rest - mid.astype(jnp.float32)).astype(jnp.bfloat16)
    return hi, mid, lo


def score_kernel(subcells, weight_ref, sub_t_ref, fc_ref, truth_ref, out_ref):
    members, rows, cells, block = (
        fc_ref.shape[0], truth_ref.shape[0], truth_ref.shape[1], fc_ref.shape[2]
    )
    total_rows = weight_ref.shape[0] // subcells
    slot = 128
    lanes = members * slot
    first = lax.axis_index("lat") * rows
    variables = cells // subcells
    cell_sub = lax.broadcasted_iota(jnp.int32, (cells, 1), 0) // variables
    pad = jnp.zeros((cells, slot - block), jnp.float32)
    for i in range(rows):
        g = first + i
        scale = jnp.zeros((cells, 1), jnp.float32)
        for s in range(subcells):
            scale = jnp.where(cell_sub == s, weight_ref[s * total_rows + g], scale)
        values = jnp.concatenate(
            [
                jnp.concatenate(
                    [fc_ref[n, i * cells : (i + 1) * cells].astype(jnp.float32), pad], axis=1
                )
                for n in range(members)
            ],
            axis=1,
        )
        truth_slot = jnp.concatenate([truth_ref[i], pad], axis=1)
        truth = jnp.concatenate([truth_slot] * members, axis=1)
        spread = jnp.zeros((cells, lanes), jnp.float32)
        for k in range(1, (members + 1) // 2):
            term = softened_sign(values - pltpu.roll(values, k * slot, 1))
            spread = spread + term - pltpu.roll(term, lanes - k * slot, 1)
        if members % 2 == 0:
            spread = spread + softened_sign(
                values - pltpu.roll(values, (members // 2) * slot, 1)
            )
        grad = scale * (softened_sign(values - truth) - spread / members)
        coarse = None
        for part in split3(grad):
            term = jnp.dot(sub_t_ref[...], part, preferred_element_type=jnp.float32)
            coarse = term if coarse is None else coarse + term
        coarse = coarse.astype(out_ref.dtype)
        for m in range(members):
            out_ref[m, i] = coarse[:, m * slot : m * slot + block]


def grad_filtered_kernel(gc_ref, slope_ref, proj_t_ref, out_ref):
    blocks, rows = gc_ref.shape[0], gc_ref.shape[1]
    width_p = slope_ref.shape[2]
    for i in range(rows):
        row = jnp.concatenate([gc_ref[q, i] for q in range(blocks)], axis=1)
        width = row.shape[1]
        extra = width_p - width
        lo = extra // 2
        hi = extra - lo
        ring = jnp.concatenate([row, row[:, :lo], row[:, width - hi :]], axis=1)
        grad_act = jnp.dot(
            proj_t_ref[...], ring.astype(jnp.float32), preferred_element_type=jnp.float32
        )
        out_ref[i] = (grad_act * slope_ref[i]).astype(jnp.bfloat16)


def backward_terms(basis_ref, step_ref, quad_ref, table_ref, rows, sources, acc):
    total_rows = step_ref.shape[0]
    first = lax.axis_index("lat") * rows
    for e, src_ref, r in sources:
        cp, width_p = src_ref.shape[1], src_ref.shape[2]
        a_lo = max(0, 2 * HALF - e)
        a_hi = min(TAPS - 1, rows - 1 + 2 * HALF - e)
        if a_lo > a_hi:
            continue
        g = jnp.clip(first - HALF + e, 0, total_rows - 1)
        step = step_ref[g]
        weights = jnp.concatenate(
            [
                jnp.concatenate(
                    [table_ref[1, basis_ref[g * TAPS * TAPS + a * TAPS + b]] for b in range(TAPS)],
                    axis=1,
                )
                for a in range(a_lo, a_hi + 1)
            ],
            axis=0,
        )
        source = src_ref[r]
        rolled = []
        for b in range(TAPS):
            if b == HALF:
                rolled.append(source)
            else:
                shift = lax.rem((b - HALF) * step + width_p, width_p)
                rolled.append(pltpu.roll(source, shift, 1))
        stacked = jnp.concatenate(rolled, axis=0)
        part = jnp.dot(weights, stacked, preferred_element_type=jnp.float32)
        scale = quad_ref[g]
        for a in range(a_lo, a_hi + 1):
            i2 = e + a - 2 * HALF
            piece = part[(a - a_lo) * cp : (a - a_lo + 1) * cp] * scale
            acc[i2] = piece if acc[i2] is None else acc[i2] + piece
    return acc


def backward_own_kernel(basis_ref, step_ref, quad_ref, own_ref, table_ref, acc_ref):
    rows = own_ref.shape[0]
    acc = backward_terms(
        basis_ref, step_ref, quad_ref, table_ref, rows,
        [(HALF + r, own_ref, r) for r in range(rows)], [None] * rows,
    )
    for i2 in range(rows):
        acc_ref[i2] = acc[i2]


def backward_prev_kernel(basis_ref, step_ref, quad_ref, prev_ref, acc_in_ref, table_ref,
                         acc_ref):
    rows = acc_in_ref.shape[0]
    acc = backward_terms(
        basis_ref, step_ref, quad_ref, table_ref, rows,
        [(e, prev_ref, e) for e in range(HALF)],
        [acc_in_ref[i2] for i2 in range(rows)],
    )
    for i2 in range(rows):
        acc_ref[i2] = acc[i2]


def backward_next_kernel(basis_ref, step_ref, quad_ref, next_ref, acc_in_ref, table_ref,
                         out_ref):
    rows = acc_in_ref.shape[0]
    channels, width = out_ref.shape[1], out_ref.shape[2]
    acc = backward_terms(
        basis_ref, step_ref, quad_ref, table_ref, rows,
        [(HALF + rows + e, next_ref, e) for e in range(HALF)],
        [acc_in_ref[i2] for i2 in range(rows)],
    )
    for i2 in range(rows):
        out_ref[i2] = acc[i2][:channels, :width].astype(out_ref.dtype)


def vmem():
    return pl.BlockSpec(memory_space=pltpu.VMEM)


def smem():
    return pl.BlockSpec(memory_space=pltpu.SMEM)


def on_device(latents, filters, project, subcell_maps, verifying_truth, basis_rows, step_rows):
    rows = latents.shape[1]
    channels = latents.shape[2]
    width = latents.shape[3]
    variables = project.shape[0]
    subcells = subcell_maps.shape[0]
    cp = round_up(channels, 16)
    vp = round_up(variables, 16)
    svp = subcells * variables
    width_p = ring_width(width)
    total_rows = rows * lax.axis_size("lat")
    first = lax.axis_index("lat") * rows

    quad_all = latitude_rows(total_rows, total_rows)
    weight_all = subcell_weight(0, total_rows, total_rows).reshape(-1)
    vq = round_up(variables, 8)
    sub_t = pad_axis(subcell_maps.reshape(subcells * variables, variables).T, 0, vq)
    blocks = lax.axis_size("member")
    block = width // blocks
    truth = verifying_truth.reshape(subcells * variables, rows, block).transpose(1, 0, 2)

    table = jnp.concatenate([filters, jnp.zeros((1,) + filters.shape[1:], filters.dtype)], 0)
    table = pad_axis(pad_axis(table, 1, cp), 2, cp)
    tables = jnp.stack([table, table.transpose(0, 2, 1)])
    basis_flat = basis_rows.reshape(-1)

    proj_p = pad_axis(pad_axis(project, 0, vp), 1, cp)
    sub_p = pad_axis(pad_axis(subcell_maps.reshape(subcells * variables, variables), 0, svp), 1, vp)

    own = to_ring(pad_axis(latents[0], 1, cp), width_p)
    low, high = halo(own, "lat", HALF)

    slope, fc = pl.pallas_call(
        forward_kernel,
        out_shape=(
            jax.ShapeDtypeStruct((rows, cp, width_p), jnp.float32),
            jax.ShapeDtypeStruct((blocks, rows * svp, block), jnp.bfloat16),
        ),
        in_specs=[smem(), smem(), smem()] + [vmem()] * 6,
        out_specs=(vmem(), vmem()),
    )(basis_flat, step_rows, quad_all, low, own, high, tables, proj_p, sub_p)

    fc_owned = lax.all_to_all(fc, "member", split_axis=0, concat_axis=0, tiled=True)
    gc_owned = pl.pallas_call(
        functools.partial(score_kernel, subcells),
        out_shape=jax.ShapeDtypeStruct((blocks, rows, vq, block), jnp.bfloat16),
        in_specs=[smem()] + [vmem()] * 3,
        out_specs=vmem(),
    )(weight_all, sub_t, fc_owned, truth)
    gc_home = lax.all_to_all(gc_owned, "member", split_axis=0, concat_axis=0, tiled=True)
    proj_t = pad_axis(pad_axis(project.T, 0, cp), 1, vq).astype(jnp.float32)
    grad_filtered = pl.pallas_call(
        grad_filtered_kernel,
        out_shape=jax.ShapeDtypeStruct((rows, cp, width_p), jnp.bfloat16),
        in_specs=[vmem()] * 3,
        out_specs=vmem(),
    )(gc_home, slope, proj_t)

    g_low, g_high = halo(grad_filtered, "lat", HALF)
    own_terms = pl.pallas_call(
        backward_own_kernel,
        out_shape=jax.ShapeDtypeStruct((rows, cp, width_p), jnp.float32),
        in_specs=[smem(), smem(), smem()] + [vmem()] * 2,
        out_specs=vmem(),
        cost_estimate=pl.CostEstimate(
            flops=2 * rows * rows * cp * TAPS * cp * width_p,
            transcendentals=0,
            bytes_accessed=rows * cp * width_p * 6,
        ),
    )(basis_flat, step_rows, quad_all, grad_filtered, tables)
    with_prev = pl.pallas_call(
        backward_prev_kernel,
        out_shape=jax.ShapeDtypeStruct((rows, cp, width_p), jnp.float32),
        in_specs=[smem(), smem(), smem()] + [vmem()] * 3,
        out_specs=vmem(),
        cost_estimate=pl.CostEstimate(
            flops=2 * rows * HALF * cp * TAPS * cp * width_p,
            transcendentals=0,
            bytes_accessed=rows * cp * width_p * 10,
        ),
    )(basis_flat, step_rows, quad_all, g_low, own_terms, tables)
    result = pl.pallas_call(
        backward_next_kernel,
        out_shape=jax.ShapeDtypeStruct((rows, channels, width), jnp.bfloat16),
        in_specs=[smem(), smem(), smem()] + [vmem()] * 3,
        out_specs=vmem(),
    )(basis_flat, step_rows, quad_all, g_high, with_prev, tables)
    return result[None]


def solution(mesh):
    placed = (
        P("member", "lat", None, None),
        P(),
        P(),
        P(),
        P(None, None, "lat", "member"),
        P(),
        P(),
    )
    return jax.shard_map(
        on_device,
        mesh=mesh,
        in_specs=placed,
        out_specs=P("member", "lat", None, None),
        check_vma=False,
    )
```

```python
import functools

import jax
import jax.numpy as jnp
from jax import lax
from jax.experimental import pallas as pl
from jax.experimental.pallas import tpu as pltpu
from jax.sharding import PartitionSpec as P

TAPS = 7
HALF = 3
MAX_STEP = 3


def round_up(value, unit):
    return (value + unit - 1) // unit * unit


def ring_width(width):
    return round_up(width + 4 * HALF * MAX_STEP + 2, 128)


def to_ring(block, width_p):
    width = block.shape[-1]
    extra = width_p - width
    lo = extra // 2
    hi = extra - lo
    return jnp.concatenate(
        [block, block[..., :lo], block[..., width - hi :]], axis=-1
    )


def pad_axis(block, axis, size):
    pads = [(0, 0)] * block.ndim
    pads[axis] = (0, size - block.shape[axis])
    return jnp.pad(block, pads)


def halo(block, axis_name, width):
    count = lax.axis_size(axis_name)
    forward = [(i, i + 1) for i in range(count - 1)]
    backward = [(target, source) for source, target in forward]
    low = lax.ppermute(block[block.shape[0] - width :], axis_name, forward)
    high = lax.ppermute(block[:width], axis_name, backward)
    return low, high


def latitude_rows(count, total):
    rows = jnp.arange(count, dtype=jnp.int32).astype(jnp.float32)
    return jnp.cos(((rows + 0.5) / total - 0.5) * jnp.pi)


def subcell_weight(first, count, total):
    rows = (first + jnp.arange(count, dtype=jnp.int32)).astype(jnp.float32)
    sub_row = jnp.array([0.0, 0.0, 1.0, 1.0], jnp.float32)
    fine = 2.0 * rows[None, :] + sub_row[:, None]
    return jnp.cos(((fine + 0.5) / (2.0 * total) - 0.5) * jnp.pi)


def softened_sign(diff):
    return diff / jnp.sqrt(diff * diff + 0.01)


SQRT_2_OVER_PI = 0.7978845608028654


def gelu(x):
    inner = SQRT_2_OVER_PI * (x + 0.044715 * (x * x * x))
    return x * (0.5 * (1.0 + jnp.tanh(inner)))


def gelu_grad(x):
    inner = SQRT_2_OVER_PI * (x + 0.044715 * (x * x * x))
    t = jnp.tanh(inner)
    d_inner = SQRT_2_OVER_PI * (1.0 + 3.0 * 0.044715 * (x * x))
    return 0.5 * (1.0 + t) + x * (0.5 * (1.0 - t * t)) * d_inner


def gelu_and_grad(x):
    inner = SQRT_2_OVER_PI * (x + 0.044715 * (x * x * x))
    t = jnp.tanh(inner)
    d_inner = SQRT_2_OVER_PI * (1.0 + 3.0 * 0.044715 * (x * x))
    half = 0.5 * (1.0 + t)
    return x * half, half + x * (0.5 * (1.0 - t * t)) * d_inner


def forward_kernel(basis_ref, step_ref, quad_ref, prev_ref, own_ref, next_ref, table_ref,
                   proj_ref, sub_ref, slope_ref, fc_ref):
    rows, cp, width_p = own_ref.shape
    first = lax.axis_index("lat") * rows
    ext = (
        [prev_ref[e] for e in range(HALF)]
        + [own_ref[e] for e in range(rows)]
        + [next_ref[e] for e in range(HALF)]
    )
    for i in range(rows):
        g = first + i
        step = step_ref[g]
        weights = jnp.concatenate(
            [
                jnp.concatenate(
                    [table_ref[0, basis_ref[g * TAPS * TAPS + a * TAPS + b]] for a in range(TAPS)],
                    axis=1,
                )
                for b in range(TAPS)
            ],
            axis=0,
        )
        stacked = jnp.concatenate(ext[i : i + TAPS], axis=0)
        taps = jnp.dot(weights, stacked, preferred_element_type=jnp.float32)
        total = taps[HALF * cp : (HALF + 1) * cp]
        for b in range(TAPS):
            if b == HALF:
                continue
            shift = lax.rem((HALF - b) * step + width_p, width_p)
            total = total + pltpu.roll(taps[b * cp : (b + 1) * cp], shift, 1)
        filtered = total * quad_ref[g]
        gelu_value, gelu_slope = gelu_and_grad(filtered)
        slope_ref[i] = gelu_slope
        activated = gelu_value.astype(jnp.bfloat16)
        coarse = jnp.dot(
            proj_ref[...], activated, preferred_element_type=jnp.float32
        ).astype(jnp.bfloat16)
        forecast = jnp.dot(
            sub_ref[...], coarse, preferred_element_type=jnp.float32
        ).astype(jnp.bfloat16)
        blocks, block = fc_ref.shape[0], fc_ref.shape[3]
        for q in range(blocks):
            fc_ref[q, i] = forecast[:, q * block : (q + 1) * block]


def split3(x):
    hi = x.astype(jnp.bfloat16)
    rest = x - hi.astype(jnp.float32)
    mid = rest.astype(jnp.bfloat16)
    lo = (rest - mid.astype(jnp.float32)).astype(jnp.bfloat16)
    return hi, mid, lo


def score_kernel(subcells, weight_ref, sub_t_ref, fc_ref, truth_ref, out_ref):
    members, rows, cells, block = fc_ref.shape
    total_rows = weight_ref.shape[0] // subcells
    slot = 128
    lanes = members * slot
    first = lax.axis_index("lat") * rows
    variables = cells // subcells
    cell_sub = lax.broadcasted_iota(jnp.int32, (cells, 1), 0) // variables
    pad = jnp.zeros((cells, slot - block), jnp.float32)
    for i in range(rows):
        g = first + i
        scale = jnp.zeros((cells, 1), jnp.float32)
        for s in range(subcells):
            scale = jnp.where(cell_sub == s, weight_ref[s * total_rows + g], scale)
        values = jnp.concatenate(
            [
                jnp.concatenate([fc_ref[n, i].astype(jnp.float32), pad], axis=1)
                for n in range(members)
            ],
            axis=1,
        )
        truth_slot = jnp.concatenate([truth_ref[i], pad], axis=1)
        truth = jnp.concatenate([truth_slot] * members, axis=1)
        spread = jnp.zeros((cells, lanes), jnp.float32)
        for k in range(1, (members + 1) // 2):
            term = softened_sign(values - pltpu.roll(values, k * slot, 1))
            spread = spread + term - pltpu.roll(term, lanes - k * slot, 1)
        if members % 2 == 0:
            spread = spread + softened_sign(
                values - pltpu.roll(values, (members // 2) * slot, 1)
            )
        grad = scale * (softened_sign(values - truth) - spread / members)
        coarse = None
        for part in split3(grad):
            term = jnp.dot(sub_t_ref[...], part, preferred_element_type=jnp.float32)
            coarse = term if coarse is None else coarse + term
        coarse = coarse.astype(out_ref.dtype)
        for m in range(members):
            out_ref[m, i] = coarse[:, m * slot : m * slot + block]


def grad_filtered_kernel(gc_ref, slope_ref, proj_t_ref, out_ref):
    blocks = gc_ref.shape[0]
    width_p = slope_ref.shape[2]
    i = pl.program_id(0)
    row = jnp.concatenate([gc_ref[q, i] for q in range(blocks)], axis=1)
    width = row.shape[1]
    extra = width_p - width
    lo = extra // 2
    hi = extra - lo
    ring = jnp.concatenate([row, row[:, :lo], row[:, width - hi :]], axis=1)
    grad_act = jnp.dot(
        proj_t_ref[...], ring.astype(jnp.float32), preferred_element_type=jnp.float32
    )
    out_ref[0] = (grad_act * slope_ref[0]).astype(jnp.bfloat16)


def backward_terms(basis_ref, step_ref, quad_ref, table_ref, rows, sources, acc):
    total_rows = step_ref.shape[0]
    first = lax.axis_index("lat") * rows
    for e, src_ref, r in sources:
        cp, width_p = src_ref.shape[1], src_ref.shape[2]
        a_lo = max(0, 2 * HALF - e)
        a_hi = min(TAPS - 1, rows - 1 + 2 * HALF - e)
        if a_lo > a_hi:
            continue
        g = jnp.clip(first - HALF + e, 0, total_rows - 1)
        step = step_ref[g]
        weights = jnp.concatenate(
            [
                jnp.concatenate(
                    [table_ref[1, basis_ref[g * TAPS * TAPS + a * TAPS + b]] for b in range(TAPS)],
                    axis=1,
                )
                for a in range(a_lo, a_hi + 1)
            ],
            axis=0,
        )
        source = src_ref[r]
        rolled = []
        for b in range(TAPS):
            if b == HALF:
                rolled.append(source)
            else:
                shift = lax.rem((b - HALF) * step + width_p, width_p)
                rolled.append(pltpu.roll(source, shift, 1))
        stacked = jnp.concatenate(rolled, axis=0)
        part = jnp.dot(weights, stacked, preferred_element_type=jnp.float32)
        scale = quad_ref[g]
        for a in range(a_lo, a_hi + 1):
            i2 = e + a - 2 * HALF
            piece = part[(a - a_lo) * cp : (a - a_lo + 1) * cp] * scale
            acc[i2] = piece if acc[i2] is None else acc[i2] + piece
    return acc


def backward_own_kernel(basis_ref, step_ref, quad_ref, own_ref, table_ref, acc_ref):
    rows = own_ref.shape[0]
    acc = backward_terms(
        basis_ref, step_ref, quad_ref, table_ref, rows,
        [(HALF + r, own_ref, r) for r in range(rows)], [None] * rows,
    )
    for i2 in range(rows):
        acc_ref[i2] = acc[i2]


def backward_prev_kernel(basis_ref, step_ref, quad_ref, prev_ref, acc_in_ref, table_ref,
                         acc_ref):
    rows = acc_in_ref.shape[0]
    acc = backward_terms(
        basis_ref, step_ref, quad_ref, table_ref, rows,
        [(e, prev_ref, e) for e in range(HALF)],
        [acc_in_ref[i2] for i2 in range(rows)],
    )
    for i2 in range(rows):
        acc_ref[i2] = acc[i2]


def backward_next_kernel(basis_ref, step_ref, quad_ref, next_ref, acc_in_ref, table_ref,
                         out_ref):
    rows = acc_in_ref.shape[0]
    channels, width = out_ref.shape[1], out_ref.shape[2]
    acc = backward_terms(
        basis_ref, step_ref, quad_ref, table_ref, rows,
        [(HALF + rows + e, next_ref, e) for e in range(HALF)],
        [acc_in_ref[i2] for i2 in range(rows)],
    )
    for i2 in range(rows):
        out_ref[i2] = acc[i2][:channels, :width].astype(out_ref.dtype)


def vmem():
    return pl.BlockSpec(memory_space=pltpu.VMEM)


def smem():
    return pl.BlockSpec(memory_space=pltpu.SMEM)


def on_device(latents, filters, project, subcell_maps, verifying_truth, basis_rows, step_rows):
    rows = latents.shape[1]
    channels = latents.shape[2]
    width = latents.shape[3]
    variables = project.shape[0]
    subcells = subcell_maps.shape[0]
    cp = round_up(channels, 16)
    vp = round_up(variables, 16)
    svp = subcells * variables
    width_p = ring_width(width)
    total_rows = rows * lax.axis_size("lat")
    first = lax.axis_index("lat") * rows

    quad_all = latitude_rows(total_rows, total_rows)
    weight_all = subcell_weight(0, total_rows, total_rows).reshape(-1)
    vq = round_up(variables, 8)
    sub_t = pad_axis(subcell_maps.reshape(subcells * variables, variables).T, 0, vq)
    blocks = lax.axis_size("member")
    block = width // blocks
    truth = verifying_truth.reshape(subcells * variables, rows, block).transpose(1, 0, 2)

    table = jnp.concatenate([filters, jnp.zeros((1,) + filters.shape[1:], filters.dtype)], 0)
    table = pad_axis(pad_axis(table, 1, cp), 2, cp)
    tables = jnp.stack([table, table.transpose(0, 2, 1)])
    basis_flat = basis_rows.reshape(-1)

    proj_p = pad_axis(pad_axis(project, 0, vp), 1, cp)
    sub_p = pad_axis(pad_axis(subcell_maps.reshape(subcells * variables, variables), 0, svp), 1, vp)

    own = to_ring(pad_axis(latents[0], 1, cp), width_p)
    low, high = halo(own, "lat", HALF)

    slope, fc = pl.pallas_call(
        forward_kernel,
        out_shape=(
            jax.ShapeDtypeStruct((rows, cp, width_p), jnp.float32),
            jax.ShapeDtypeStruct((blocks, rows, svp, block), jnp.bfloat16),
        ),
        in_specs=[smem(), smem(), smem()] + [vmem()] * 6,
        out_specs=(vmem(), vmem()),
    )(basis_flat, step_rows, quad_all, low, own, high, tables, proj_p, sub_p)

    fc_owned = lax.all_to_all(fc, "member", split_axis=0, concat_axis=0, tiled=True)
    gc_owned = pl.pallas_call(
        functools.partial(score_kernel, subcells),
        out_shape=jax.ShapeDtypeStruct((blocks, rows, vq, block), jnp.bfloat16),
        in_specs=[smem()] + [vmem()] * 3,
        out_specs=vmem(),
    )(weight_all, sub_t, fc_owned, truth)
    gc_home = lax.all_to_all(gc_owned, "member", split_axis=0, concat_axis=0, tiled=True)
    proj_t = pad_axis(pad_axis(project.T, 0, cp), 1, vq).astype(jnp.float32)
    grad_filtered = pl.pallas_call(
        grad_filtered_kernel,
        out_shape=jax.ShapeDtypeStruct((rows, cp, width_p), jnp.bfloat16),
        grid=(rows,),
        in_specs=[
            pl.BlockSpec(gc_home.shape, lambda i: (0, 0, 0, 0)),
            pl.BlockSpec((1, cp, width_p), lambda i: (i, 0, 0)),
            pl.BlockSpec(proj_t.shape, lambda i: (0, 0)),
        ],
        out_specs=pl.BlockSpec((1, cp, width_p), lambda i: (i, 0, 0)),
    )(gc_home, slope, proj_t)

    g_low, g_high = halo(grad_filtered, "lat", HALF)
    own_terms = pl.pallas_call(
        backward_own_kernel,
        out_shape=jax.ShapeDtypeStruct((rows, cp, width_p), jnp.float32),
        in_specs=[smem(), smem(), smem()] + [vmem()] * 2,
        out_specs=vmem(),
        cost_estimate=pl.CostEstimate(
            flops=2 * rows * rows * cp * TAPS * cp * width_p,
            transcendentals=0,
            bytes_accessed=rows * cp * width_p * 6,
        ),
    )(basis_flat, step_rows, quad_all, grad_filtered, tables)
    with_prev = pl.pallas_call(
        backward_prev_kernel,
        out_shape=jax.ShapeDtypeStruct((rows, cp, width_p), jnp.float32),
        in_specs=[smem(), smem(), smem()] + [vmem()] * 3,
        out_specs=vmem(),
        cost_estimate=pl.CostEstimate(
            flops=2 * rows * HALF * cp * TAPS * cp * width_p,
            transcendentals=0,
            bytes_accessed=rows * cp * width_p * 10,
        ),
    )(basis_flat, step_rows, quad_all, g_low, own_terms, tables)
    result = pl.pallas_call(
        backward_next_kernel,
        out_shape=jax.ShapeDtypeStruct((rows, channels, width), jnp.bfloat16),
        in_specs=[smem(), smem(), smem()] + [vmem()] * 3,
        out_specs=vmem(),
    )(basis_flat, step_rows, quad_all, g_high, with_prev, tables)
    return result[None]


def solution(mesh):
    placed = (
        P("member", "lat", None, None),
        P(),
        P(),
        P(),
        P(None, None, "lat", "member"),
        P(),
        P(),
    )
    return jax.shard_map(
        on_device,
        mesh=mesh,
        in_specs=placed,
        out_specs=P("member", "lat", None, None),
        check_vma=False,
    )
```

```python
import functools

import jax
import jax.numpy as jnp
from jax import lax
from jax.experimental import pallas as pl
from jax.experimental.pallas import tpu as pltpu
from jax.sharding import PartitionSpec as P

TAPS = 7
HALF = 3
MAX_STEP = 3


def round_up(value, unit):
    return (value + unit - 1) // unit * unit


def ring_width(width):
    return round_up(width + 4 * HALF * MAX_STEP + 2, 128)


def to_ring(block, width_p):
    width = block.shape[-1]
    extra = width_p - width
    lo = extra // 2
    hi = extra - lo
    return jnp.concatenate(
        [block, block[..., :lo], block[..., width - hi :]], axis=-1
    )


def pad_axis(block, axis, size):
    pads = [(0, 0)] * block.ndim
    pads[axis] = (0, size - block.shape[axis])
    return jnp.pad(block, pads)


def halo(block, axis_name, width):
    count = lax.axis_size(axis_name)
    forward = [(i, i + 1) for i in range(count - 1)]
    backward = [(target, source) for source, target in forward]
    low = lax.ppermute(block[block.shape[0] - width :], axis_name, forward)
    high = lax.ppermute(block[:width], axis_name, backward)
    return low, high


def latitude_rows(count, total):
    rows = jnp.arange(count, dtype=jnp.int32).astype(jnp.float32)
    return jnp.cos(((rows + 0.5) / total - 0.5) * jnp.pi)


def subcell_weight(first, count, total):
    rows = (first + jnp.arange(count, dtype=jnp.int32)).astype(jnp.float32)
    sub_row = jnp.array([0.0, 0.0, 1.0, 1.0], jnp.float32)
    fine = 2.0 * rows[None, :] + sub_row[:, None]
    return jnp.cos(((fine + 0.5) / (2.0 * total) - 0.5) * jnp.pi)


def softened_sign(diff):
    return diff / jnp.sqrt(diff * diff + 0.01)


SQRT_2_OVER_PI = 0.7978845608028654


def gelu(x):
    inner = SQRT_2_OVER_PI * (x + 0.044715 * (x * x * x))
    return x * (0.5 * (1.0 + jnp.tanh(inner)))


def gelu_grad(x):
    inner = SQRT_2_OVER_PI * (x + 0.044715 * (x * x * x))
    t = jnp.tanh(inner)
    d_inner = SQRT_2_OVER_PI * (1.0 + 3.0 * 0.044715 * (x * x))
    return 0.5 * (1.0 + t) + x * (0.5 * (1.0 - t * t)) * d_inner


def gelu_and_grad(x):
    inner = SQRT_2_OVER_PI * (x + 0.044715 * (x * x * x))
    t = jnp.tanh(inner)
    d_inner = SQRT_2_OVER_PI * (1.0 + 3.0 * 0.044715 * (x * x))
    half = 0.5 * (1.0 + t)
    return x * half, half + x * (0.5 * (1.0 - t * t)) * d_inner


def forward_kernel(basis_ref, step_ref, quad_ref, prev_ref, own_ref, next_ref, table_ref,
                   proj_ref, sub_ref, slope_ref, fc_ref):
    rows, cp, width_p = own_ref.shape
    first = lax.axis_index("lat") * rows
    ext = (
        [prev_ref[e] for e in range(HALF)]
        + [own_ref[e] for e in range(rows)]
        + [next_ref[e] for e in range(HALF)]
    )
    for i in range(rows):
        g = first + i
        step = step_ref[g]
        weights = jnp.concatenate(
            [
                jnp.concatenate(
                    [table_ref[0, basis_ref[g * TAPS * TAPS + a * TAPS + b]] for a in range(TAPS)],
                    axis=1,
                )
                for b in range(TAPS)
            ],
            axis=0,
        )
        stacked = jnp.concatenate(ext[i : i + TAPS], axis=0)
        taps = jnp.dot(weights, stacked, preferred_element_type=jnp.float32)
        total = taps[HALF * cp : (HALF + 1) * cp]
        for b in range(TAPS):
            if b == HALF:
                continue
            shift = lax.rem((HALF - b) * step + width_p, width_p)
            total = total + pltpu.roll(taps[b * cp : (b + 1) * cp], shift, 1)
        filtered = total * quad_ref[g]
        gelu_value, gelu_slope = gelu_and_grad(filtered)
        slope_ref[i] = gelu_slope
        activated = gelu_value.astype(jnp.bfloat16)
        coarse = jnp.dot(
            proj_ref[...], activated, preferred_element_type=jnp.float32
        ).astype(jnp.bfloat16)
        forecast = jnp.dot(
            sub_ref[...], coarse, preferred_element_type=jnp.float32
        ).astype(jnp.bfloat16)
        blocks, block = fc_ref.shape[0], fc_ref.shape[3]
        for q in range(blocks):
            fc_ref[q, i] = forecast[:, q * block : (q + 1) * block]


def split3(x):
    hi = x.astype(jnp.bfloat16)
    rest = x - hi.astype(jnp.float32)
    mid = rest.astype(jnp.bfloat16)
    lo = (rest - mid.astype(jnp.float32)).astype(jnp.bfloat16)
    return hi, mid, lo


def score_kernel(subcells, weight_ref, sub_t_ref, fc_ref, truth_ref, out_ref):
    members, rows, cells, block = fc_ref.shape
    total_rows = weight_ref.shape[0] // subcells
    slot = 128
    lanes = members * slot
    first = lax.axis_index("lat") * rows
    variables = cells // subcells
    cell_sub = lax.broadcasted_iota(jnp.int32, (cells, 1), 0) // variables
    pad = jnp.zeros((cells, slot - block), jnp.float32)
    for i in range(rows):
        g = first + i
        scale = jnp.zeros((cells, 1), jnp.float32)
        for s in range(subcells):
            scale = jnp.where(cell_sub == s, weight_ref[s * total_rows + g], scale)
        values = jnp.concatenate(
            [
                jnp.concatenate([fc_ref[n, i].astype(jnp.float32), pad], axis=1)
                for n in range(members)
            ],
            axis=1,
        )
        truth_slot = jnp.concatenate([truth_ref[i], pad], axis=1)
        truth = jnp.concatenate([truth_slot] * members, axis=1)
        spread = jnp.zeros((cells, lanes), jnp.float32)
        for k in range(1, (members + 1) // 2):
            term = softened_sign(values - pltpu.roll(values, k * slot, 1))
            spread = spread + term - pltpu.roll(term, lanes - k * slot, 1)
        if members % 2 == 0:
            spread = spread + softened_sign(
                values - pltpu.roll(values, (members // 2) * slot, 1)
            )
        grad = scale * (softened_sign(values - truth) - spread / members)
        coarse = None
        for part in split3(grad):
            term = jnp.dot(sub_t_ref[...], part, preferred_element_type=jnp.float32)
            coarse = term if coarse is None else coarse + term
        coarse = coarse.astype(out_ref.dtype)
        for m in range(members):
            out_ref[m, i] = coarse[:, m * slot : m * slot + block]


def grad_filtered_kernel(gc_ref, slope_ref, proj_t_ref, out_ref):
    blocks, rows = gc_ref.shape[0], gc_ref.shape[1]
    width_p = slope_ref.shape[2]
    for i in range(rows):
        row = jnp.concatenate([gc_ref[q, i] for q in range(blocks)], axis=1)
        width = row.shape[1]
        extra = width_p - width
        lo = extra // 2
        hi = extra - lo
        ring = jnp.concatenate([row, row[:, :lo], row[:, width - hi :]], axis=1)
        grad_act = jnp.dot(
            proj_t_ref[...], ring, preferred_element_type=jnp.float32
        )
        out_ref[i] = (grad_act * slope_ref[i]).astype(jnp.bfloat16)


def backward_terms(basis_ref, step_ref, quad_ref, table_ref, rows, sources, acc):
    total_rows = step_ref.shape[0]
    first = lax.axis_index("lat") * rows
    for e, src_ref, r in sources:
        cp, width_p = src_ref.shape[1], src_ref.shape[2]
        a_lo = max(0, 2 * HALF - e)
        a_hi = min(TAPS - 1, rows - 1 + 2 * HALF - e)
        if a_lo > a_hi:
            continue
        g = jnp.clip(first - HALF + e, 0, total_rows - 1)
        step = step_ref[g]
        weights = jnp.concatenate(
            [
                jnp.concatenate(
                    [table_ref[1, basis_ref[g * TAPS * TAPS + a * TAPS + b]] for b in range(TAPS)],
                    axis=1,
                )
                for a in range(a_lo, a_hi + 1)
            ],
            axis=0,
        )
        source = src_ref[r]
        rolled = []
        for b in range(TAPS):
            if b == HALF:
                rolled.append(source)
            else:
                shift = lax.rem((b - HALF) * step + width_p, width_p)
                rolled.append(pltpu.roll(source, shift, 1))
        stacked = jnp.concatenate(rolled, axis=0)
        part = jnp.dot(weights, stacked, preferred_element_type=jnp.float32)
        scale = quad_ref[g]
        for a in range(a_lo, a_hi + 1):
            i2 = e + a - 2 * HALF
            piece = part[(a - a_lo) * cp : (a - a_lo + 1) * cp] * scale
            acc[i2] = piece if acc[i2] is None else acc[i2] + piece
    return acc


def backward_own_kernel(basis_ref, step_ref, quad_ref, own_ref, table_ref, acc_ref):
    rows = own_ref.shape[0]
    acc = backward_terms(
        basis_ref, step_ref, quad_ref, table_ref, rows,
        [(HALF + r, own_ref, r) for r in range(rows)], [None] * rows,
    )
    for i2 in range(rows):
        acc_ref[i2] = acc[i2]


def backward_prev_kernel(basis_ref, step_ref, quad_ref, prev_ref, acc_in_ref, table_ref,
                         acc_ref):
    rows = acc_in_ref.shape[0]
    acc = backward_terms(
        basis_ref, step_ref, quad_ref, table_ref, rows,
        [(e, prev_ref, e) for e in range(HALF)],
        [acc_in_ref[i2] for i2 in range(rows)],
    )
    for i2 in range(rows):
        acc_ref[i2] = acc[i2]


def backward_next_kernel(basis_ref, step_ref, quad_ref, next_ref, acc_in_ref, table_ref,
                         out_ref):
    rows = acc_in_ref.shape[0]
    channels, width = out_ref.shape[1], out_ref.shape[2]
    acc = backward_terms(
        basis_ref, step_ref, quad_ref, table_ref, rows,
        [(HALF + rows + e, next_ref, e) for e in range(HALF)],
        [acc_in_ref[i2] for i2 in range(rows)],
    )
    for i2 in range(rows):
        out_ref[i2] = acc[i2][:channels, :width].astype(out_ref.dtype)


def vmem():
    return pl.BlockSpec(memory_space=pltpu.VMEM)


def smem():
    return pl.BlockSpec(memory_space=pltpu.SMEM)


def on_device(latents, filters, project, subcell_maps, verifying_truth, basis_rows, step_rows):
    rows = latents.shape[1]
    channels = latents.shape[2]
    width = latents.shape[3]
    variables = project.shape[0]
    subcells = subcell_maps.shape[0]
    cp = round_up(channels, 16)
    vp = round_up(variables, 16)
    svp = subcells * variables
    width_p = ring_width(width)
    total_rows = rows * lax.axis_size("lat")
    first = lax.axis_index("lat") * rows

    quad_all = latitude_rows(total_rows, total_rows)
    weight_all = subcell_weight(0, total_rows, total_rows).reshape(-1)
    vq = round_up(variables, 8)
    sub_t = pad_axis(subcell_maps.reshape(subcells * variables, variables).T, 0, vq)
    blocks = lax.axis_size("member")
    block = width // blocks
    truth = verifying_truth.reshape(subcells * variables, rows, block).transpose(1, 0, 2)

    table = jnp.concatenate([filters, jnp.zeros((1,) + filters.shape[1:], filters.dtype)], 0)
    table = pad_axis(pad_axis(table, 1, cp), 2, cp)
    tables = jnp.stack([table, table.transpose(0, 2, 1)])
    basis_flat = basis_rows.reshape(-1)

    proj_p = pad_axis(pad_axis(project, 0, vp), 1, cp)
    sub_p = pad_axis(pad_axis(subcell_maps.reshape(subcells * variables, variables), 0, svp), 1, vp)

    own = to_ring(pad_axis(latents[0], 1, cp), width_p)
    low, high = halo(own, "lat", HALF)

    slope, fc = pl.pallas_call(
        forward_kernel,
        out_shape=(
            jax.ShapeDtypeStruct((rows, cp, width_p), jnp.float32),
            jax.ShapeDtypeStruct((blocks, rows, svp, block), jnp.bfloat16),
        ),
        in_specs=[smem(), smem(), smem()] + [vmem()] * 6,
        out_specs=(vmem(), vmem()),
    )(basis_flat, step_rows, quad_all, low, own, high, tables, proj_p, sub_p)

    fc_owned = lax.all_to_all(fc, "member", split_axis=0, concat_axis=0, tiled=True)
    gc_owned = pl.pallas_call(
        functools.partial(score_kernel, subcells),
        out_shape=jax.ShapeDtypeStruct((blocks, rows, vq, block), jnp.bfloat16),
        in_specs=[smem()] + [vmem()] * 3,
        out_specs=vmem(),
    )(weight_all, sub_t, fc_owned, truth)
    gc_home = lax.all_to_all(gc_owned, "member", split_axis=0, concat_axis=0, tiled=True)
    proj_t = pad_axis(pad_axis(project.T, 0, cp), 1, vq)
    grad_filtered = pl.pallas_call(
        grad_filtered_kernel,
        out_shape=jax.ShapeDtypeStruct((rows, cp, width_p), jnp.bfloat16),
        in_specs=[vmem()] * 3,
        out_specs=vmem(),
    )(gc_home, slope, proj_t)

    g_low, g_high = halo(grad_filtered, "lat", HALF)
    own_terms = pl.pallas_call(
        backward_own_kernel,
        out_shape=jax.ShapeDtypeStruct((rows, cp, width_p), jnp.float32),
        in_specs=[smem(), smem(), smem()] + [vmem()] * 2,
        out_specs=vmem(),
        cost_estimate=pl.CostEstimate(
            flops=2 * rows * rows * cp * TAPS * cp * width_p,
            transcendentals=0,
            bytes_accessed=rows * cp * width_p * 6,
        ),
    )(basis_flat, step_rows, quad_all, grad_filtered, tables)
    with_prev = pl.pallas_call(
        backward_prev_kernel,
        out_shape=jax.ShapeDtypeStruct((rows, cp, width_p), jnp.float32),
        in_specs=[smem(), smem(), smem()] + [vmem()] * 3,
        out_specs=vmem(),
        cost_estimate=pl.CostEstimate(
            flops=2 * rows * HALF * cp * TAPS * cp * width_p,
            transcendentals=0,
            bytes_accessed=rows * cp * width_p * 10,
        ),
    )(basis_flat, step_rows, quad_all, g_low, own_terms, tables)
    result = pl.pallas_call(
        backward_next_kernel,
        out_shape=jax.ShapeDtypeStruct((rows, channels, width), jnp.bfloat16),
        in_specs=[smem(), smem(), smem()] + [vmem()] * 3,
        out_specs=vmem(),
    )(basis_flat, step_rows, quad_all, g_high, with_prev, tables)
    return result[None]


def solution(mesh):
    placed = (
        P("member", "lat", None, None),
        P(),
        P(),
        P(),
        P(None, None, "lat", "member"),
        P(),
        P(),
    )
    return jax.shard_map(
        on_device,
        mesh=mesh,
        in_specs=placed,
        out_specs=P("member", "lat", None, None),
        check_vma=False,
    )
```
